256 devices in a mesh: section: 4 (over z_hi, core), ep: 64 (over y, x, z_lo).
Axes of the slice: x: 4, y: 4, z: 8 (z_hi: 2, z_lo: 4; z = z_hi * 4 + z_lo), core: 2. Of those that a mesh axis runs over, the one named last changes fastest.
Arguments:
- tokens: bfloat16 [4, 8192, 4096], P('section', 'ep'), may hold values from -6 to 6
- routes: int32 [4, 8192, 8], P('section', 'ep'), may hold values from 0 to 127, as said below
- router_weights: float32 [4, 8192, 8], P('section', 'ep'), may hold values from 0.25 to 1
- w_gate: bfloat16 [4, 64, 4096, 384], P('section', 'ep'), may hold values from -0.09375 to 0.09375
- w_up: bfloat16 [4, 64, 4096, 384], P('section', 'ep'), may hold values from -0.09375 to 0.09375
- w_down: bfloat16 [4, 64, 384, 4096], P('section', 'ep'), may hold values from -0.15625 to 0.15625
- w_query: bfloat16 [4, 4096, 1024], P('section', 'ep'), may hold values from -0.09375 to 0.09375
- w_keyval: bfloat16 [4, 4096, 256], P('section', 'ep'), may hold values from -0.09375 to 0.09375
- gain_query: float32 [4, 128], P('section'), may hold values from 0.8 to 2
- gain_key: float32 [4, 128], P('section'), may hold values from 0.8 to 2
- segment_ids: int32 [4, 8192], P('section', 'ep'), may hold values from 0 to 31, never falling along the last dimension, each value on 1 to 512 neighbouring positions
Outputs:
- layer_out: bfloat16 [4, 8192, 4096], P('section', 'ep')
- attended: bfloat16 [4, 8192, 1024], P('section', 'ep')
The draws below stay inside these ranges and needn't reach their ends.
Inputs may be any that keep to these rules, and one draw needn't show every extreme that they name: `routes`: each token names 8 different experts, at most one of them below 16. Among the tokens of one device (aligned blocks of 128 rows in each section) no expert below 16 is named by more than 8 of them, and in each section one expert below 16 is named by exactly 8 tokens of every block. `segment_ids`: along each section's tokens the reaction numbers never fall; each reaction spans 1 to 512 tokens and one spans exactly 512.
All inputs are finite; a program needn't handle non-finite values.
Results may differ from the reference program's by a relative error of at most 0.018.
Values may be sent and summed in bfloat16 or wider, within the bound.
No kernel may reach another device: no remote copies, remote signals or barrier semaphores. Data moves between devices by JAX's collectives and lax.ppermute only.
A program may use at most 128 MiB of HBM per device.

```python
import math
import jax
import jax.numpy as jnp
import numpy as np
from jax import lax

D = 4096
HID = 1536
EXPERTS = 128
TOPK = 8
HD = 128
QH = 8
OWNERS = 4
SEG_MOST = 512
TOK_DEV = 128
SECTIONS = 4
TOKENS = 8192
SEGMENTS = 32
EXP_FLY = 16
CAP = 8
HID_PART = 384
N_EP = 64


def draw_routes(key, part):
    per_section = TOKENS // TOK_DEV
    blocks = SECTIONS * per_section
    subkeys = jax.random.split(jax.random.fold_in(key, 11), 7)
    hot_expert = jax.random.randint(subkeys[0], (SECTIONS, 1), 0, EXP_FLY)
    hot_expert = jnp.broadcast_to(hot_expert, (SECTIONS, per_section)).reshape(blocks)
    shuffled = jax.vmap(lambda subkey: jax.random.permutation(subkey, TOK_DEV))(jax.random.split(subkeys[1], blocks))
    forced = shuffled < CAP
    other_expert = (hot_expert[:, None] + 1 + jax.random.randint(subkeys[2], (blocks, TOK_DEV), 0, EXP_FLY - 1)) % EXP_FLY
    wants_route = (jax.random.randint(subkeys[3], (blocks, TOK_DEV), 0, 2) == 1) & jnp.logical_not(forced)
    expert_ids = jnp.arange(EXP_FLY, dtype=jnp.int32)
    onehot = ((other_expert[..., None] == expert_ids) & wants_route[..., None]).astype(jnp.int32)
    rank_before = jnp.sum((jnp.cumsum(onehot, axis=1) - onehot) * onehot, axis=-1)
    kept_route = wants_route & (rank_before < CAP)
    has_route = forced | kept_route
    held_expert = jnp.where(forced, hot_expert[:, None], other_expert)
    outside_span = EXPERTS - EXP_FLY
    stride = outside_span // TOPK
    start_at = jax.random.randint(subkeys[4], (blocks, TOK_DEV, 1), 0, outside_span)
    jitter = jax.random.randint(subkeys[5], (blocks, TOK_DEV, TOPK), 0, stride)
    outside = EXP_FLY + (start_at + jnp.arange(TOPK, dtype=jnp.int32) * stride + jitter) % outside_span
    placed_at = jax.random.randint(subkeys[6], (blocks, TOK_DEV, 1), 0, TOPK)
    selected = (jnp.arange(TOPK, dtype=jnp.int32) == placed_at) & has_route[..., None]
    routes = jnp.where(selected, held_expert[..., None], outside)
    return routes.reshape(SECTIONS, TOKENS, TOPK).astype(jnp.int32)


def shard_levels(key, dims, cuts, least, top_value):
    level = 1.0
    for axis_at, parts in cuts:
        steps = jax.random.uniform(jax.random.fold_in(jax.random.fold_in(key, 6), axis_at), (parts,), jnp.float32, least / len(cuts), top_value / len(cuts))
        level = level * jnp.repeat(jnp.exp(steps), dims[axis_at] // parts).reshape((-1,) + (1,) * (len(dims) - 1 - axis_at))
    return level


def profile(amount, total, limit, slope):
    weights = [(1 << 20) // math.isqrt(grade ** slope) + 1 for grade in range(2, amount + 1)]
    spare, counts = total - limit - (amount - 1), [1] * (amount - 1)
    while spare > 0:
        candidates = [i for i in range(amount - 1) if counts[i] < limit]
        pool, left = sum([weights[i] for i in candidates]), spare
        for i in candidates:
            more = min(limit - counts[i], max(1, left * weights[i] // pool), spare)
            counts[i] = counts[i] + more
            spare = spare - more
    return np.array([limit] + counts)


def ragged(stream_key, number_of, total, limit, skew):
    if number_of == 2:
        one = jax.random.randint(stream_key, (), max(1, total - limit), min(limit, total - 1) + 1)
        return jnp.stack([one, total - one])
    lengths = jnp.asarray(profile(number_of, total, limit, skew), jnp.int32)
    twos = (number_of - 1) // 2
    source_of, taker = lengths[1:1 + 2 * twos:2], lengths[2:2 + 2 * twos:2]
    margin = jnp.minimum(source_of - 1, limit - taker)
    moved = jax.random.randint(jax.random.fold_in(stream_key, 1), (twos,), 0, 1 << 20) % (margin + 1)
    lengths = lengths.at[1:1 + 2 * twos:2].set(source_of - moved).at[2:2 + 2 * twos:2].set(taker + moved)
    return lengths[jax.random.permutation(jax.random.fold_in(stream_key, 2), number_of)]


def gaussian(key, extent, deviation, bound, shards=(), kind=jnp.bfloat16):
    gain = shard_levels(key, extent, shards, -0.22, 0.18) if shards else 1.0
    result = jax.random.normal(key, extent, jnp.float32) * deviation * gain
    return jnp.minimum(jnp.maximum(result, -bound), bound).astype(kind)


def setup_inputs(seed: int = 0) -> dict:
    arg_keys = jax.random.split(jax.random.key(seed), 12)
    tokens = gaussian(arg_keys[0], (SECTIONS, TOKENS, D), 1.0, 6.0, ((0, 4), (1, 64)))
    routes = draw_routes(jax.random.fold_in(arg_keys[11], 71), 0)
    router_weights = jnp.clip(0.25 + 0.75 * jax.random.uniform(arg_keys[2], (SECTIONS, TOKENS, TOPK), jnp.float32) ** shard_levels(arg_keys[2], (SECTIONS, TOKENS, TOPK), ((0, 4), (1, 64)), -0.2, 0.2), 0.25, 1.0)
    w_gate = gaussian(arg_keys[3], (SECTIONS, EXP_FLY * OWNERS, D, HID_PART), D ** -0.5, 0.09375, ((0, 4), (1, 64)))
    w_up = gaussian(arg_keys[4], (SECTIONS, EXP_FLY * OWNERS, D, HID_PART), D ** -0.5, 0.09375, ((0, 4), (1, 64)))
    w_down = gaussian(arg_keys[5], (SECTIONS, EXP_FLY * OWNERS, HID_PART, D), HID ** -0.5, 0.15625, ((0, 4), (1, 64)))
    w_query = gaussian(arg_keys[6], (SECTIONS, D, QH * HD), D ** -0.5, 0.09375, ((0, 4), (1, 64)))
    w_keyval = gaussian(arg_keys[7], (SECTIONS, D, 2 * HD), D ** -0.5, 0.09375, ((0, 4), (1, 64)))
    gain_query = jnp.clip(jnp.exp(math.log(2.0) - 0.9162907 * jax.random.uniform(arg_keys[8], (SECTIONS, HD), jnp.float32) ** shard_levels(arg_keys[8], (SECTIONS, HD), ((0, 4),), -0.2, 0.2)), 0.8, 2.0)
    gain_key = jnp.clip(jnp.exp(math.log(2.0) - 0.9162907 * jax.random.uniform(arg_keys[9], (SECTIONS, HD), jnp.float32) ** shard_levels(arg_keys[9], (SECTIONS, HD), ((0, 4),), -0.2, 0.2)), 0.8, 2.0)
    segment_ids = jax.vmap(lambda own: jnp.searchsorted(jnp.cumsum(ragged(own, SEGMENTS, TOKENS, SEG_MOST, 1)), jnp.arange(TOKENS), side="right"))(jax.random.split(arg_keys[10], SECTIONS)).reshape((SECTIONS, TOKENS)).astype(jnp.int32)
    return {"tokens": tokens, "routes": routes, "router_weights": router_weights, "w_gate": w_gate, "w_up": w_up, "w_down": w_down, "w_query": w_query, "w_keyval": w_keyval, "gain_query": gain_query, "gain_key": gain_key, "segment_ids": segment_ids}


EPSILON = 1e-06
ROPE_BASE = 1000000.0

def rms_rows(values):
    return values * lax.rsqrt(lax.optimization_barrier(jnp.mean(values * values, axis=-1, keepdims=True)) + EPSILON)

def rotary(values, position):
    half_count = values.shape[-1] // 2
    frequency = ROPE_BASE ** (-(jnp.arange(half_count, dtype=jnp.float32) * 2.0) / values.shape[-1])
    angles = position.astype(jnp.float32)[:, None] * frequency[None, :]
    cosine = jnp.concatenate([jnp.cos(angles), jnp.cos(angles)], axis=-1)[:, None, :]
    sine = jnp.concatenate([jnp.sin(angles), jnp.sin(angles)], axis=-1)[:, None, :]
    turned = jnp.concatenate([-values[..., half_count:], values[..., :half_count]], axis=-1)
    return values * cosine + turned * sine

def expert_layer(tokens, routes, router_weights, w_gate, w_up, w_down):
    wide_tokens = tokens.astype(jnp.float32)
    normed = rms_rows(wide_tokens).astype(jnp.bfloat16)
    inside = routes < EXP_FLY
    has_route = jnp.any(inside, axis=-1)
    chosen = lax.optimization_barrier(jnp.sum(jnp.where(inside, routes, 0), axis=-1)).astype(jnp.int32)
    weight_kept = lax.optimization_barrier(jnp.sum(jnp.where(inside, router_weights, 0.0), axis=-1))
    gate_all = w_gate.reshape(EXP_FLY, OWNERS, D, HID_PART).transpose(0, 2, 1, 3).reshape(EXP_FLY, D, HID)
    up_all = w_up.reshape(EXP_FLY, OWNERS, D, HID_PART).transpose(0, 2, 1, 3).reshape(EXP_FLY, D, HID)
    down_all = w_down.reshape(EXP_FLY, HID, D)

    def one_expert(running, expert_index):
        member = has_route & (chosen == expert_index)
        row_ids = jnp.nonzero(member, size=N_EP * CAP, fill_value=0)[0]
        live_rows = jnp.arange(N_EP * CAP) < jnp.sum(member)
        picked = normed[row_ids]
        gate_proj = jnp.dot(picked, gate_all[expert_index], preferred_element_type=jnp.float32)
        up_proj = jnp.dot(picked, up_all[expert_index], preferred_element_type=jnp.float32)
        activated = (jax.nn.silu(gate_proj) * up_proj).astype(jnp.bfloat16)
        expert_rows = jnp.dot(activated, down_all[expert_index], preferred_element_type=jnp.float32)
        return (running.at[row_ids].add(jnp.where(live_rows[:, None], expert_rows, 0.0)), None)
    expert_out, _ = lax.scan(one_expert, jnp.zeros((TOKENS, D), jnp.float32), jnp.arange(EXP_FLY, dtype=jnp.int32))
    return (wide_tokens + weight_kept[:, None] * expert_out).astype(jnp.bfloat16)

def attention(arrived, w_query, w_keyval, gain_query, gain_key, segment_row):
    lifted = rms_rows(arrived.astype(jnp.float32)).astype(jnp.bfloat16)
    query_raw = jnp.dot(lifted, w_query, preferred_element_type=jnp.float32).reshape(TOKENS, QH, HD)
    keyval_raw = jnp.dot(lifted, w_keyval, preferred_element_type=jnp.float32)
    index_all = jnp.arange(TOKENS, dtype=jnp.int32)
    change = jnp.concatenate([jnp.ones((1,), dtype=bool), segment_row[1:] != segment_row[:-1]])
    starts = lax.cummax(jnp.where(change, index_all, 0).astype(jnp.int32), axis=0).astype(jnp.int32)
    position = (index_all - starts).astype(jnp.int32)
    query = rotary(rms_rows(query_raw) * gain_query, position).astype(jnp.bfloat16)
    key_part = rotary(rms_rows(keyval_raw[:, None, :HD]) * gain_key, position)[:, 0].astype(jnp.bfloat16)
    value_part = keyval_raw[:, HD:].astype(jnp.bfloat16)
    key_wide = lax.optimization_barrier(key_part).astype(jnp.float32)
    value_wide = lax.optimization_barrier(value_part).astype(jnp.float32)
    query_kept = lax.optimization_barrier(query)
    block_rows = math.gcd(TOKENS, 512)
    score_scale = 1.0 / math.sqrt(HD)

    def one_block(block_index):
        first_row = (block_index * block_rows).astype(jnp.int32)
        query_block = lax.dynamic_slice_in_dim(query_kept, first_row, block_rows, 0).astype(jnp.float32)
        query_start = lax.dynamic_slice_in_dim(starts, first_row, block_rows, 0)
        scores = jnp.einsum('qhd,kd->qhk', query_block, key_wide) * score_scale
        query_pos = first_row + jnp.arange(block_rows, dtype=jnp.int32)
        allowed = (index_all[None, None, :] <= query_pos[:, None, None]) & (index_all[None, None, :] >= query_start[:, None, None])
        probabilities = jnp.where(allowed, jnp.exp(scores), 0.0)
        total_mass = lax.optimization_barrier(jnp.sum(probabilities, axis=-1))
        rounded = lax.optimization_barrier(probabilities.astype(jnp.bfloat16)).astype(jnp.float32)
        mixed = jnp.einsum('qhk,kd->qhd', rounded, value_wide) / total_mass[..., None]
        return mixed.astype(jnp.bfloat16).reshape(block_rows, QH * HD)
    return lax.map(one_block, jnp.arange(TOKENS // block_rows, dtype=jnp.int32)).reshape(TOKENS, QH * HD)

def reference(tokens, routes, router_weights, w_gate, w_up, w_down, w_query, w_keyval, gain_query, gain_key, segment_ids):
    section_outs = []
    for section_index in range(SECTIONS):
        section_outs.append(expert_layer(tokens[section_index], routes[section_index], router_weights[section_index], w_gate[section_index], w_up[section_index], w_down[section_index]))
    section_attended = []
    for section_index in range(SECTIONS):
        previous = section_outs[(section_index - 1) % SECTIONS]
        section_attended.append(attention(previous, w_query[section_index], w_keyval[section_index], gain_query[section_index], gain_key[section_index], segment_ids[section_index]))
    return (jnp.stack(section_outs), jnp.stack(section_attended))
```

```python
import math

import jax
import jax.numpy as jnp
from jax import lax
from jax.sharding import PartitionSpec as P

OWNERS = 4
SEG_MOST = 512


EPSILON = 1e-06
ROPE_BASE = 1000000.0
FAR_INDEX = 1073741824


def passed_along(block, axis, distance):
    devices = range(lax.axis_size(axis))
    route = [((i - distance) % len(devices), i) for i in devices]
    return lax.ppermute(block, axis, route)


def prefix(shard, axis, combine, identity):
    length, mine = (lax.axis_size(axis), lax.axis_index(axis))
    everything = jax.tree.map(lambda part: lax.all_gather(part, axis), shard)
    start = jax.tree.map(
        lambda part, zero: jnp.broadcast_to(jnp.asarray(zero, part.dtype), part.shape),
        shard,
        identity,
    )

    def step(k, before):
        reached = k < mine
        new = combine(before, jax.tree.map(lambda part: part[k], everything))
        return jax.tree.map(lambda a, b: jnp.where(reached, a, b), new, before)

    return lax.fori_loop(0, length, step, start)


def passed_along_2(value, axis, steps):
    count = lax.axis_size(axis)
    leading, last = (max(0, -steps), min(count, count - steps))
    return lax.ppermute(value, axis, [(source, source + steps) for source in range(leading, last)])


def rms_rows(values):
    return values * lax.rsqrt(jnp.mean(values * values, axis=-1, keepdims=True) + EPSILON)


def rotary(values, position):
    half_count = values.shape[-1] // 2
    frequency = ROPE_BASE ** (-(jnp.arange(half_count, dtype=jnp.float32) * 2.0) / values.shape[-1])
    angles = position.astype(jnp.float32)[:, None] * frequency[None, :]
    cosine = jnp.concatenate([jnp.cos(angles), jnp.cos(angles)], axis=-1)[:, None, :]
    sine = jnp.concatenate([jnp.sin(angles), jnp.sin(angles)], axis=-1)[:, None, :]
    turned = jnp.concatenate([-values[..., half_count:], values[..., :half_count]], axis=-1)
    return values * cosine + turned * sine


def feed_forward(row_block, gate_part, up_part, down_part):
    gate_proj = jnp.dot(row_block, gate_part, preferred_element_type=jnp.float32)
    up_proj = jnp.dot(row_block, up_part, preferred_element_type=jnp.float32)
    activated = (jax.nn.silu(gate_proj) * up_proj).astype(jnp.bfloat16)
    return jnp.dot(activated, down_part, preferred_element_type=jnp.float32)


def keep_later(earlier, later):
    same_id = earlier[0] == later[0]
    newer_id = later[0] > earlier[0]
    start_at = jnp.where(
        same_id, jnp.minimum(earlier[1], later[1]), jnp.where(newer_id, later[1], earlier[1])
    )
    return (jnp.maximum(earlier[0], later[0]), start_at)


def on_device(
    tokens,
    routes,
    router_weights,
    w_gate,
    w_up,
    w_down,
    w_query,
    w_keyval,
    gain_query,
    gain_key,
    segment_ids,
):
    device_count = lax.axis_size("ep")
    expert_count = device_count // OWNERS
    token_count = tokens.shape[1]
    model_width = tokens.shape[2]
    capacity = OWNERS * max(1, token_count // device_count)
    wide_tokens = tokens[0].astype(jnp.float32)
    normed = rms_rows(wide_tokens).astype(jnp.bfloat16)
    inside = routes[0] < expert_count
    has_route = jnp.any(inside, axis=-1)
    chosen = jnp.sum(jnp.where(inside, routes[0], 0), axis=-1)
    weight_kept = jnp.sum(jnp.where(inside, router_weights[0], 0.0), axis=-1)
    expert_ids = jnp.arange(expert_count, dtype=jnp.int32)
    member = ((chosen[:, None] == expert_ids[None, :]) & has_route[:, None]).astype(jnp.int32)
    rank_within = jnp.sum((jnp.cumsum(member, axis=0) - member) * member, axis=-1)
    slot_index = jnp.where(has_route, chosen * capacity + rank_within, -1)
    slot_ids = jnp.arange(expert_count * capacity, dtype=jnp.int32)
    placing = (slot_ids[:, None] == slot_index[None, :]).astype(jnp.bfloat16)
    packed = jnp.dot(placing, normed, preferred_element_type=jnp.float32).astype(jnp.bfloat16)
    gate_part = w_gate[0, 0]
    up_part = w_up[0, 0]
    down_part = w_down[0, 0]
    spread = jnp.broadcast_to(
        packed.reshape(expert_count, 1, capacity, model_width),
        (expert_count, OWNERS, capacity, model_width),
    ).reshape(device_count, capacity, model_width)
    received = lax.all_to_all(spread, "ep", split_axis=0, concat_axis=0, tiled=True)
    partial_out = feed_forward(
        received.reshape(-1, model_width), gate_part, up_part, down_part
    ).reshape(received.shape)
    returned_rows = lax.all_to_all(
        partial_out.astype(jnp.bfloat16), "ep", split_axis=0, concat_axis=0, tiled=True
    ).astype(partial_out.dtype)
    merged = jnp.sum(
        returned_rows.reshape(expert_count, OWNERS, capacity, model_width), axis=1
    ).reshape(expert_count * capacity, model_width)
    fetched_rows = jnp.take(merged, jnp.maximum(slot_index, 0), axis=0)
    expert_out = jnp.where(has_route[:, None], fetched_rows, 0.0)
    layer_out = (wide_tokens + weight_kept[:, None] * expert_out).astype(jnp.bfloat16)
    arrived = passed_along(layer_out, "section", 1)
    lifted = rms_rows(arrived.astype(jnp.float32)).astype(jnp.bfloat16)
    head_dim = gain_query.shape[-1]
    query_width = w_query.shape[-1]
    head_count = query_width // head_dim
    query_raw = jnp.dot(
        lifted,
        lax.all_gather(w_query[0], "ep", axis=0, tiled=True),
        preferred_element_type=jnp.float32,
    )
    keyval_raw = jnp.dot(
        lifted,
        lax.all_gather(w_keyval[0], "ep", axis=0, tiled=True),
        preferred_element_type=jnp.float32,
    )
    segment_row = segment_ids[0]
    first_index = lax.axis_index("ep") * token_count
    global_index = first_index + jnp.arange(token_count, dtype=jnp.int32)
    reach = (SEG_MOST - 1) // token_count + 1
    key_index = (
        first_index - reach * token_count + jnp.arange((reach + 1) * token_count, dtype=jnp.int32)
    )
    segment_pieces = []
    for distance in range(1, reach + 1):
        segment_pieces.append(passed_along_2(segment_row, "ep", distance))
    window_segment = jnp.concatenate(segment_pieces[::-1] + [segment_row], axis=0)
    window_segment = jnp.where(key_index >= 0, window_segment, -1)
    same_segment = window_segment[None, :] == segment_row[:, None]
    start_index = jnp.min(jnp.where(same_segment, key_index[None, :], FAR_INDEX), axis=1)
    position = global_index - start_index
    query = rotary(
        rms_rows(query_raw.reshape(token_count, head_count, head_dim)) * gain_query[0], position
    ).astype(jnp.bfloat16)
    key_part = rotary(rms_rows(keyval_raw[:, None, :head_dim]) * gain_key[0], position)[
        :, 0
    ].astype(jnp.bfloat16)
    value_part = keyval_raw[:, head_dim:].astype(jnp.bfloat16)
    key_value = jnp.concatenate([key_part, value_part], axis=-1)
    earlier_pieces = []
    for distance in range(1, reach + 1):
        earlier_pieces.append(passed_along_2(key_value, "ep", distance))
    window = jnp.concatenate(earlier_pieces[::-1] + [key_value], axis=0)
    score_scale = 1.0 / math.sqrt(head_dim)
    scores = (
        jnp.einsum(
            "thd,kd->thk", query, window[:, :head_dim], preferred_element_type=jnp.float32
        )
        * score_scale
    )
    allowed = (same_segment & (key_index[None, :] <= global_index[:, None]))[:, None, :]
    probabilities = jnp.where(allowed, jnp.exp(scores), 0.0)
    total_mass = jnp.sum(probabilities, axis=-1)
    mixed = jnp.einsum(
        "thk,kd->thd",
        probabilities.astype(jnp.bfloat16),
        window[:, head_dim:],
        preferred_element_type=jnp.float32,
    )
    attended = (mixed / total_mass[..., None]).astype(jnp.bfloat16).reshape(token_count, query_width)
    return (layer_out[None], attended[None])


def solution(mesh):
    in_specs = (
        P("section", "ep", None),
        P("section", "ep", None),
        P("section", "ep", None),
        P("section", "ep", None, None),
        P("section", "ep", None, None),
        P("section", "ep", None, None),
        P("section", "ep", None),
        P("section", "ep", None),
        P("section", None),
        P("section", None),
        P("section", "ep"),
    )
    out_specs = (P("section", "ep", None), P("section", "ep", None))
    return jax.shard_map(
        on_device, mesh=mesh, in_specs=in_specs, out_specs=out_specs, check_vma=False
    )
```

```python
import math

import jax
import jax.numpy as jnp
from jax import lax
from jax.sharding import PartitionSpec as P

OWNERS = 4
SEG_MOST = 512


EPSILON = 1e-06
ROPE_BASE = 1000000.0
FAR_INDEX = 1073741824
EP = ("ep_y", "ep_x", "ep_z")


def passed_along(block, axis, distance):
    devices = range(lax.axis_size(axis))
    route = [((i - distance) % len(devices), i) for i in devices]
    return lax.ppermute(block, axis, route)


def prefix(shard, axis, combine, identity):
    length, mine = (lax.axis_size(axis), lax.axis_index(axis))
    everything = jax.tree.map(lambda part: lax.all_gather(part, axis), shard)
    start = jax.tree.map(
        lambda part, zero: jnp.broadcast_to(jnp.asarray(zero, part.dtype), part.shape),
        shard,
        identity,
    )

    def step(k, before):
        reached = k < mine
        new = combine(before, jax.tree.map(lambda part: part[k], everything))
        return jax.tree.map(lambda a, b: jnp.where(reached, a, b), new, before)

    return lax.fori_loop(0, length, step, start)


def passed_along_2(value, axis, steps):
    count = lax.axis_size(axis)
    leading, last = (max(0, -steps), min(count, count - steps))
    return lax.ppermute(value, axis, [(source, source + steps) for source in range(leading, last)])


def rms_rows(values):
    return values * lax.rsqrt(jnp.mean(values * values, axis=-1, keepdims=True) + EPSILON)


def rotary(values, position):
    half_count = values.shape[-1] // 2
    frequency = ROPE_BASE ** (-(jnp.arange(half_count, dtype=jnp.float32) * 2.0) / values.shape[-1])
    angles = position.astype(jnp.float32)[:, None] * frequency[None, :]
    cosine = jnp.concatenate([jnp.cos(angles), jnp.cos(angles)], axis=-1)[:, None, :]
    sine = jnp.concatenate([jnp.sin(angles), jnp.sin(angles)], axis=-1)[:, None, :]
    turned = jnp.concatenate([-values[..., half_count:], values[..., :half_count]], axis=-1)
    return values * cosine + turned * sine


def feed_forward(row_block, gate_part, up_part, down_part):
    gate_proj = jnp.dot(row_block, gate_part, preferred_element_type=jnp.float32)
    up_proj = jnp.dot(row_block, up_part, preferred_element_type=jnp.float32)
    activated = (jax.nn.silu(gate_proj) * up_proj).astype(jnp.bfloat16)
    return jnp.dot(activated, down_part, preferred_element_type=jnp.float32)


def keep_later(earlier, later):
    same_id = earlier[0] == later[0]
    newer_id = later[0] > earlier[0]
    start_at = jnp.where(
        same_id, jnp.minimum(earlier[1], later[1]), jnp.where(newer_id, later[1], earlier[1])
    )
    return (jnp.maximum(earlier[0], later[0]), start_at)


def on_device(
    tokens,
    routes,
    router_weights,
    w_gate,
    w_up,
    w_down,
    w_query,
    w_keyval,
    gain_query,
    gain_key,
    segment_ids,
):
    device_count = lax.axis_size(EP)
    expert_count = device_count // OWNERS
    token_count = tokens.shape[1]
    model_width = tokens.shape[2]
    capacity = OWNERS * max(1, token_count // device_count)
    wide_tokens = tokens[0].astype(jnp.float32)
    normed = rms_rows(wide_tokens).astype(jnp.bfloat16)
    inside = routes[0] < expert_count
    has_route = jnp.any(inside, axis=-1)
    chosen = jnp.sum(jnp.where(inside, routes[0], 0), axis=-1)
    weight_kept = jnp.sum(jnp.where(inside, router_weights[0], 0.0), axis=-1)
    expert_ids = jnp.arange(expert_count, dtype=jnp.int32)
    member = ((chosen[:, None] == expert_ids[None, :]) & has_route[:, None]).astype(jnp.int32)
    rank_within = jnp.sum((jnp.cumsum(member, axis=0) - member) * member, axis=-1)
    slot_index = jnp.where(has_route, chosen * capacity + rank_within, -1)
    slot_ids = jnp.arange(expert_count * capacity, dtype=jnp.int32)
    placing = (slot_ids[:, None] == slot_index[None, :]).astype(jnp.bfloat16)
    packed = jnp.dot(placing, normed, preferred_element_type=jnp.float32).astype(jnp.bfloat16)
    gate_part = w_gate[0, 0]
    up_part = w_up[0, 0]
    down_part = w_down[0, 0]
    spread = jnp.broadcast_to(
        packed.reshape(expert_count, 1, capacity, model_width),
        (expert_count, OWNERS, capacity, model_width),
    ).reshape(device_count, capacity, model_width)
    received = lax.all_to_all(spread, EP, split_axis=0, concat_axis=0, tiled=True)
    partial_out = feed_forward(
        received.reshape(-1, model_width), gate_part, up_part, down_part
    ).reshape(received.shape)
    returned_rows = lax.all_to_all(
        partial_out.astype(jnp.bfloat16), EP, split_axis=0, concat_axis=0, tiled=True
    ).astype(partial_out.dtype)
    merged = jnp.sum(
        returned_rows.reshape(expert_count, OWNERS, capacity, model_width), axis=1
    ).reshape(expert_count * capacity, model_width)
    fetched_rows = jnp.take(merged, jnp.maximum(slot_index, 0), axis=0)
    expert_out = jnp.where(has_route[:, None], fetched_rows, 0.0)
    layer_out = (wide_tokens + weight_kept[:, None] * expert_out).astype(jnp.bfloat16)
    arrived = passed_along(layer_out, "section", 1)
    lifted = rms_rows(arrived.astype(jnp.float32)).astype(jnp.bfloat16)
    head_dim = gain_query.shape[-1]
    query_width = w_query.shape[-1]
    head_count = query_width // head_dim
    projection = jnp.concatenate([w_query[0], w_keyval[0]], axis=-1)
    for axis in EP[::-1]:
        projection = lax.all_gather(projection, axis, axis=0, tiled=True)
    projected = jnp.dot(lifted, projection, preferred_element_type=jnp.float32)
    query_raw = projected[:, :query_width]
    keyval_raw = projected[:, query_width:]
    segment_row = segment_ids[0]
    first_index = lax.axis_index(EP) * token_count
    global_index = first_index + jnp.arange(token_count, dtype=jnp.int32)
    reach = (SEG_MOST - 1) // token_count + 1
    key_index = (
        first_index - reach * token_count + jnp.arange((reach + 1) * token_count, dtype=jnp.int32)
    )
    segment_pieces = []
    for distance in range(1, reach + 1):
        segment_pieces.append(passed_along_2(segment_row, EP, distance))
    window_segment = jnp.concatenate(segment_pieces[::-1] + [segment_row], axis=0)
    window_segment = jnp.where(key_index >= 0, window_segment, -1)
    same_segment = window_segment[None, :] == segment_row[:, None]
    start_index = jnp.min(jnp.where(same_segment, key_index[None, :], FAR_INDEX), axis=1)
    position = global_index - start_index
    query = rotary(
        rms_rows(query_raw.reshape(token_count, head_count, head_dim)) * gain_query[0], position
    ).astype(jnp.bfloat16)
    key_part = rotary(rms_rows(keyval_raw[:, None, :head_dim]) * gain_key[0], position)[
        :, 0
    ].astype(jnp.bfloat16)
    value_part = keyval_raw[:, head_dim:].astype(jnp.bfloat16)
    key_value = jnp.concatenate([key_part, value_part], axis=-1)
    earlier_pieces = []
    for distance in range(1, reach + 1):
        earlier_pieces.append(passed_along_2(key_value, EP, distance))
    window = jnp.concatenate(earlier_pieces[::-1] + [key_value], axis=0)
    score_scale = 1.0 / math.sqrt(head_dim)
    scores = (
        jnp.einsum(
            "thd,kd->thk", query, window[:, :head_dim], preferred_element_type=jnp.float32
        )
        * score_scale
    )
    allowed = (same_segment & (key_index[None, :] <= global_index[:, None]))[:, None, :]
    probabilities = jnp.where(allowed, jnp.exp(scores), 0.0)
    total_mass = jnp.sum(probabilities, axis=-1)
    mixed = jnp.einsum(
        "thk,kd->thd",
        probabilities.astype(jnp.bfloat16),
        window[:, head_dim:],
        preferred_element_type=jnp.float32,
    )
    attended = (mixed / total_mass[..., None]).astype(jnp.bfloat16).reshape(token_count, query_width)
    return (layer_out[None], attended[None])


def solution(mesh):
    ep_size = mesh.shape["ep"]
    z_size = 4 if ep_size % 4 == 0 else 1
    x_size = 4 if ep_size % (z_size * 4) == 0 else 1
    split_mesh = jax.sharding.Mesh(
        mesh.devices.reshape(
            mesh.shape["section"], ep_size // (x_size * z_size), x_size, z_size
        ),
        ("section",) + EP,
    )
    in_specs = (
        P("section", EP, None),
        P("section", EP, None),
        P("section", EP, None),
        P("section", EP, None, None),
        P("section", EP, None, None),
        P("section", EP, None, None),
        P("section", EP, None),
        P("section", EP, None),
        P("section", None),
        P("section", None),
        P("section", EP),
    )
    out_specs = (P("section", EP, None), P("section", EP, None))
    return jax.shard_map(
        on_device, mesh=split_mesh, in_specs=in_specs, out_specs=out_specs, check_vma=False
    )
```

```python
import math

import jax
import jax.numpy as jnp
from jax import lax
from jax.sharding import PartitionSpec as P

OWNERS = 4
SEG_MOST = 512


EPSILON = 1e-06
ROPE_BASE = 1000000.0
FAR_INDEX = 1073741824
EP = ("ep_y", "ep_x", "ep_z")


def passed_along(block, axis, distance):
    devices = range(lax.axis_size(axis))
    route = [((i - distance) % len(devices), i) for i in devices]
    return lax.ppermute(block, axis, route)


def prefix(shard, axis, combine, identity):
    length, mine = (lax.axis_size(axis), lax.axis_index(axis))
    everything = jax.tree.map(lambda part: lax.all_gather(part, axis), shard)
    start = jax.tree.map(
        lambda part, zero: jnp.broadcast_to(jnp.asarray(zero, part.dtype), part.shape),
        shard,
        identity,
    )

    def step(k, before):
        reached = k < mine
        new = combine(before, jax.tree.map(lambda part: part[k], everything))
        return jax.tree.map(lambda a, b: jnp.where(reached, a, b), new, before)

    return lax.fori_loop(0, length, step, start)


def passed_along_2(value, axis, steps):
    count = lax.axis_size(axis)
    leading, last = (max(0, -steps), min(count, count - steps))
    return lax.ppermute(value, axis, [(source, source + steps) for source in range(leading, last)])


def rms_rows(values):
    return values * lax.rsqrt(jnp.mean(values * values, axis=-1, keepdims=True) + EPSILON)


def rotary(values, position):
    half_count = values.shape[-1] // 2
    frequency = ROPE_BASE ** (-(jnp.arange(half_count, dtype=jnp.float32) * 2.0) / values.shape[-1])
    angles = position.astype(jnp.float32)[:, None] * frequency[None, :]
    cosine = jnp.concatenate([jnp.cos(angles), jnp.cos(angles)], axis=-1)[:, None, :]
    sine = jnp.concatenate([jnp.sin(angles), jnp.sin(angles)], axis=-1)[:, None, :]
    turned = jnp.concatenate([-values[..., half_count:], values[..., :half_count]], axis=-1)
    return values * cosine + turned * sine


def feed_forward(row_block, gate_part, up_part, down_part):
    gate_proj = jnp.dot(row_block, gate_part, preferred_element_type=jnp.float32)
    up_proj = jnp.dot(row_block, up_part, preferred_element_type=jnp.float32)
    activated = (jax.nn.silu(gate_proj) * up_proj).astype(jnp.bfloat16)
    return jnp.dot(activated, down_part, preferred_element_type=jnp.float32)


def keep_later(earlier, later):
    same_id = earlier[0] == later[0]
    newer_id = later[0] > earlier[0]
    start_at = jnp.where(
        same_id, jnp.minimum(earlier[1], later[1]), jnp.where(newer_id, later[1], earlier[1])
    )
    return (jnp.maximum(earlier[0], later[0]), start_at)


def on_device(
    tokens,
    routes,
    router_weights,
    w_gate,
    w_up,
    w_down,
    w_query,
    w_keyval,
    gain_query,
    gain_key,
    segment_ids,
):
    device_count = lax.axis_size(EP)
    expert_count = device_count // OWNERS
    token_count = tokens.shape[1]
    model_width = tokens.shape[2]
    capacity = OWNERS * max(1, token_count // device_count)
    wide_tokens = tokens[0].astype(jnp.float32)
    normed = rms_rows(wide_tokens).astype(jnp.bfloat16)
    inside = routes[0] < expert_count
    has_route = jnp.any(inside, axis=-1)
    chosen = jnp.sum(jnp.where(inside, routes[0], 0), axis=-1)
    weight_kept = jnp.sum(jnp.where(inside, router_weights[0], 0.0), axis=-1)
    expert_ids = jnp.arange(expert_count, dtype=jnp.int32)
    member = ((chosen[:, None] == expert_ids[None, :]) & has_route[:, None]).astype(jnp.int32)
    rank_within = jnp.sum((jnp.cumsum(member, axis=0) - member) * member, axis=-1)
    slot_index = jnp.where(has_route, chosen * capacity + rank_within, -1)
    slot_ids = jnp.arange(expert_count * capacity, dtype=jnp.int32)
    placing = (slot_ids[:, None] == slot_index[None, :]).astype(jnp.bfloat16)
    packed = jnp.dot(placing, normed, preferred_element_type=jnp.float32).astype(jnp.bfloat16)
    gate_part = w_gate[0, 0]
    up_part = w_up[0, 0]
    down_part = w_down[0, 0]
    spread = jnp.broadcast_to(
        packed.reshape(expert_count, 1, capacity, model_width),
        (expert_count, OWNERS, capacity, model_width),
    ).reshape(device_count, capacity, model_width)
    segment_row = segment_ids[0]
    first_index = lax.axis_index(EP) * token_count
    reach = (SEG_MOST - 1) // token_count + 1
    segment_pieces = []
    for distance in range(1, reach + 1):
        segment_pieces.append(passed_along_2(segment_row, EP, distance))
    projection = jnp.concatenate([w_query[0], w_keyval[0]], axis=-1)
    projection = lax.all_gather(projection, EP[-1], axis=0, tiled=True)
    spread, projection, segment_pieces = lax.optimization_barrier(
        (spread, projection, segment_pieces)
    )
    projection = lax.all_gather(projection, EP[:-1], axis=0, tiled=True)
    received = lax.all_to_all(spread, EP, split_axis=0, concat_axis=0, tiled=True)
    partial_out = feed_forward(
        received.reshape(-1, model_width), gate_part, up_part, down_part
    ).reshape(received.shape)
    returned_rows = lax.all_to_all(
        partial_out.astype(jnp.bfloat16), EP, split_axis=0, concat_axis=0, tiled=True
    ).astype(partial_out.dtype)
    merged = jnp.sum(
        returned_rows.reshape(expert_count, OWNERS, capacity, model_width), axis=1
    ).reshape(expert_count * capacity, model_width)
    fetched_rows = jnp.take(merged, jnp.maximum(slot_index, 0), axis=0)
    expert_out = jnp.where(has_route[:, None], fetched_rows, 0.0)
    layer_out = (wide_tokens + weight_kept[:, None] * expert_out).astype(jnp.bfloat16)
    arrived = passed_along(layer_out, "section", 1)
    lifted = rms_rows(arrived.astype(jnp.float32)).astype(jnp.bfloat16)
    head_dim = gain_query.shape[-1]
    query_width = w_query.shape[-1]
    head_count = query_width // head_dim
    projected = jnp.dot(lifted, projection, preferred_element_type=jnp.float32)
    query_raw = projected[:, :query_width]
    keyval_raw = projected[:, query_width:]
    global_index = first_index + jnp.arange(token_count, dtype=jnp.int32)
    key_index = (
        first_index - reach * token_count + jnp.arange((reach + 1) * token_count, dtype=jnp.int32)
    )
    window_segment = jnp.concatenate(segment_pieces[::-1] + [segment_row], axis=0)
    window_segment = jnp.where(key_index >= 0, window_segment, -1)
    same_segment = window_segment[None, :] == segment_row[:, None]
    start_index = jnp.min(jnp.where(same_segment, key_index[None, :], FAR_INDEX), axis=1)
    position = global_index - start_index
    query = rotary(
        rms_rows(query_raw.reshape(token_count, head_count, head_dim)) * gain_query[0], position
    ).astype(jnp.bfloat16)
    key_part = rotary(rms_rows(keyval_raw[:, None, :head_dim]) * gain_key[0], position)[
        :, 0
    ].astype(jnp.bfloat16)
    value_part = keyval_raw[:, head_dim:].astype(jnp.bfloat16)
    key_value = jnp.concatenate([key_part, value_part], axis=-1)
    earlier_pieces = []
    for distance in range(1, reach + 1):
        earlier_pieces.append(passed_along_2(key_value, EP, distance))
    window = jnp.concatenate(earlier_pieces[::-1] + [key_value], axis=0)
    score_scale = 1.0 / math.sqrt(head_dim)
    scores = (
        jnp.einsum(
            "thd,kd->thk", query, window[:, :head_dim], preferred_element_type=jnp.float32
        )
        * score_scale
    )
    allowed = (same_segment & (key_index[None, :] <= global_index[:, None]))[:, None, :]
    probabilities = jnp.where(allowed, jnp.exp(scores), 0.0)
    total_mass = jnp.sum(probabilities, axis=-1)
    mixed = jnp.einsum(
        "thk,kd->thd",
        probabilities.astype(jnp.bfloat16),
        window[:, head_dim:],
        preferred_element_type=jnp.float32,
    )
    attended = (mixed / total_mass[..., None]).astype(jnp.bfloat16).reshape(token_count, query_width)
    return (layer_out[None], attended[None])


def solution(mesh):
    ep_size = mesh.shape["ep"]
    z_size = 4 if ep_size % 4 == 0 else 1
    x_size = 4 if ep_size % (z_size * 4) == 0 else 1
    split_mesh = jax.sharding.Mesh(
        mesh.devices.reshape(
            mesh.shape["section"], ep_size // (x_size * z_size), x_size, z_size
        ),
        ("section",) + EP,
    )
    in_specs = (
        P("section", EP, None),
        P("section", EP, None),
        P("section", EP, None),
        P("section", EP, None, None),
        P("section", EP, None, None),
        P("section", EP, None, None),
        P("section", EP, None),
        P("section", EP, None),
        P("section", None),
        P("section", None),
        P("section", EP),
    )
    out_specs = (P("section", EP, None), P("section", EP, None))
    return jax.shard_map(
        on_device, mesh=split_mesh, in_specs=in_specs, out_specs=out_specs, check_vma=False
    )
```

```python
import math

import jax
import jax.numpy as jnp
from jax import lax
from jax.sharding import PartitionSpec as P

OWNERS = 4
SEG_MOST = 512


EPSILON = 1e-06
ROPE_BASE = 1000000.0
FAR_INDEX = 1073741824
EP = ("ep_y", "ep_x", "ep_z")


def passed_along(block, axis, distance):
    devices = range(lax.axis_size(axis))
    route = [((i - distance) % len(devices), i) for i in devices]
    return lax.ppermute(block, axis, route)


def prefix(shard, axis, combine, identity):
    length, mine = (lax.axis_size(axis), lax.axis_index(axis))
    everything = jax.tree.map(lambda part: lax.all_gather(part, axis), shard)
    start = jax.tree.map(
        lambda part, zero: jnp.broadcast_to(jnp.asarray(zero, part.dtype), part.shape),
        shard,
        identity,
    )

    def step(k, before):
        reached = k < mine
        new = combine(before, jax.tree.map(lambda part: part[k], everything))
        return jax.tree.map(lambda a, b: jnp.where(reached, a, b), new, before)

    return lax.fori_loop(0, length, step, start)


def passed_along_2(value, axis, steps):
    count = lax.axis_size(axis)
    leading, last = (max(0, -steps), min(count, count - steps))
    return lax.ppermute(value, axis, [(source, source + steps) for source in range(leading, last)])


def rms_rows(values):
    return values * lax.rsqrt(jnp.mean(values * values, axis=-1, keepdims=True) + EPSILON)


def rotary(values, position):
    half_count = values.shape[-1] // 2
    frequency = ROPE_BASE ** (-(jnp.arange(half_count, dtype=jnp.float32) * 2.0) / values.shape[-1])
    angles = position.astype(jnp.float32)[:, None] * frequency[None, :]
    cosine = jnp.concatenate([jnp.cos(angles), jnp.cos(angles)], axis=-1)[:, None, :]
    sine = jnp.concatenate([jnp.sin(angles), jnp.sin(angles)], axis=-1)[:, None, :]
    turned = jnp.concatenate([-values[..., half_count:], values[..., :half_count]], axis=-1)
    return values * cosine + turned * sine


def feed_forward(row_block, gate_part, up_part, down_part):
    gate_proj = jnp.dot(row_block, gate_part, preferred_element_type=jnp.float32)
    up_proj = jnp.dot(row_block, up_part, preferred_element_type=jnp.float32)
    activated = (jax.nn.silu(gate_proj) * up_proj).astype(jnp.bfloat16)
    return jnp.dot(activated, down_part, preferred_element_type=jnp.float32)


def keep_later(earlier, later):
    same_id = earlier[0] == later[0]
    newer_id = later[0] > earlier[0]
    start_at = jnp.where(
        same_id, jnp.minimum(earlier[1], later[1]), jnp.where(newer_id, later[1], earlier[1])
    )
    return (jnp.maximum(earlier[0], later[0]), start_at)


def on_device(
    tokens,
    routes,
    router_weights,
    w_gate,
    w_up,
    w_down,
    w_query,
    w_keyval,
    gain_query,
    gain_key,
    segment_ids,
):
    device_count = lax.axis_size(EP)
    expert_count = device_count // OWNERS
    token_count = tokens.shape[1]
    model_width = tokens.shape[2]
    capacity = OWNERS * max(1, token_count // device_count)
    wide_tokens = tokens[0].astype(jnp.float32)
    normed = rms_rows(wide_tokens).astype(jnp.bfloat16)
    inside = routes[0] < expert_count
    has_route = jnp.any(inside, axis=-1)
    chosen = jnp.sum(jnp.where(inside, routes[0], 0), axis=-1)
    weight_kept = jnp.sum(jnp.where(inside, router_weights[0], 0.0), axis=-1)
    expert_ids = jnp.arange(expert_count, dtype=jnp.int32)
    member = ((chosen[:, None] == expert_ids[None, :]) & has_route[:, None]).astype(jnp.int32)
    rank_within = jnp.sum((jnp.cumsum(member, axis=0) - member) * member, axis=-1)
    slot_index = jnp.where(has_route, chosen * capacity + rank_within, -1)
    slot_ids = jnp.arange(expert_count * capacity, dtype=jnp.int32)
    placing = (slot_ids[:, None] == slot_index[None, :]).astype(jnp.bfloat16)
    packed = jnp.dot(placing, normed, preferred_element_type=jnp.float32).astype(jnp.bfloat16)
    gate_part = w_gate[0, 0]
    up_part = w_up[0, 0]
    down_part = w_down[0, 0]
    segment_row = segment_ids[0]
    first_index = lax.axis_index(EP) * token_count
    reach = (SEG_MOST - 1) // token_count + 1
    segment_pieces = []
    for distance in range(1, reach + 1):
        segment_pieces.append(passed_along_2(segment_row, EP, distance))
    projection = jnp.concatenate([w_query[0], w_keyval[0]], axis=-1)
    projection = lax.all_gather(projection, EP[-1], axis=0, tiled=True)
    packed, projection, segment_pieces = lax.optimization_barrier(
        (packed, projection, segment_pieces)
    )
    projection = lax.all_gather(projection, EP[:-1], axis=0, tiled=True)
    group_axes, owner_axis = EP[:-1], EP[-1]
    crossed = lax.all_to_all(
        packed.reshape(expert_count, capacity, model_width),
        group_axes,
        split_axis=0,
        concat_axis=0,
        tiled=True,
    )
    received = lax.all_gather(crossed, owner_axis, axis=0, tiled=True)
    partial_out = feed_forward(received, gate_part, up_part, down_part)
    reduced = lax.psum_scatter(
        partial_out.astype(jnp.bfloat16), owner_axis, scatter_dimension=0, tiled=True
    )
    merged = lax.all_to_all(
        reduced.reshape(expert_count, capacity, model_width),
        group_axes,
        split_axis=0,
        concat_axis=0,
        tiled=True,
    ).astype(jnp.float32).reshape(expert_count * capacity, model_width)
    fetched_rows = jnp.take(merged, jnp.maximum(slot_index, 0), axis=0)
    expert_out = jnp.where(has_route[:, None], fetched_rows, 0.0)
    layer_out = (wide_tokens + weight_kept[:, None] * expert_out).astype(jnp.bfloat16)
    arrived = passed_along(layer_out, "section", 1)
    lifted = rms_rows(arrived.astype(jnp.float32)).astype(jnp.bfloat16)
    head_dim = gain_query.shape[-1]
    query_width = w_query.shape[-1]
    head_count = query_width // head_dim
    projected = jnp.dot(lifted, projection, preferred_element_type=jnp.float32)
    query_raw = projected[:, :query_width]
    keyval_raw = projected[:, query_width:]
    global_index = first_index + jnp.arange(token_count, dtype=jnp.int32)
    key_index = (
        first_index - reach * token_count + jnp.arange((reach + 1) * token_count, dtype=jnp.int32)
    )
    window_segment = jnp.concatenate(segment_pieces[::-1] + [segment_row], axis=0)
    window_segment = jnp.where(key_index >= 0, window_segment, -1)
    same_segment = window_segment[None, :] == segment_row[:, None]
    start_index = jnp.min(jnp.where(same_segment, key_index[None, :], FAR_INDEX), axis=1)
    position = global_index - start_index
    query = rotary(
        rms_rows(query_raw.reshape(token_count, head_count, head_dim)) * gain_query[0], position
    ).astype(jnp.bfloat16)
    key_part = rotary(rms_rows(keyval_raw[:, None, :head_dim]) * gain_key[0], position)[
        :, 0
    ].astype(jnp.bfloat16)
    value_part = keyval_raw[:, head_dim:].astype(jnp.bfloat16)
    key_value = jnp.concatenate([key_part, value_part], axis=-1)
    earlier_pieces = []
    for distance in range(1, reach + 1):
        earlier_pieces.append(passed_along_2(key_value, EP, distance))
    window = jnp.concatenate(earlier_pieces[::-1] + [key_value], axis=0)
    score_scale = 1.0 / math.sqrt(head_dim)
    scores = (
        jnp.einsum(
            "thd,kd->thk", query, window[:, :head_dim], preferred_element_type=jnp.float32
        )
        * score_scale
    )
    allowed = (same_segment & (key_index[None, :] <= global_index[:, None]))[:, None, :]
    probabilities = jnp.where(allowed, jnp.exp(scores), 0.0)
    total_mass = jnp.sum(probabilities, axis=-1)
    mixed = jnp.einsum(
        "thk,kd->thd",
        probabilities.astype(jnp.bfloat16),
        window[:, head_dim:],
        preferred_element_type=jnp.float32,
    )
    attended = (mixed / total_mass[..., None]).astype(jnp.bfloat16).reshape(token_count, query_width)
    return (layer_out[None], attended[None])


def solution(mesh):
    ep_size = mesh.shape["ep"]
    z_size = 4 if ep_size % 4 == 0 else 1
    x_size = 4 if ep_size % (z_size * 4) == 0 else 1
    split_mesh = jax.sharding.Mesh(
        mesh.devices.reshape(
            mesh.shape["section"], ep_size // (x_size * z_size), x_size, z_size
        ),
        ("section",) + EP,
    )
    in_specs = (
        P("section", EP, None),
        P("section", EP, None),
        P("section", EP, None),
        P("section", EP, None, None),
        P("section", EP, None, None),
        P("section", EP, None, None),
        P("section", EP, None),
        P("section", EP, None),
        P("section", None),
        P("section", None),
        P("section", EP),
    )
    out_specs = (P("section", EP, None), P("section", EP, None))
    return jax.shard_map(
        on_device, mesh=split_mesh, in_specs=in_specs, out_specs=out_specs, check_vma=False
    )
```

```python
import math

import jax
import jax.numpy as jnp
from jax import lax
from jax.sharding import PartitionSpec as P

OWNERS = 4
SEG_MOST = 512


EPSILON = 1e-06
ROPE_BASE = 1000000.0
FAR_INDEX = 1073741824
EP = ("ep_y", "ep_x", "ep_z")


def passed_along(block, axis, distance):
    devices = range(lax.axis_size(axis))
    route = [((i - distance) % len(devices), i) for i in devices]
    return lax.ppermute(block, axis, route)


def prefix(shard, axis, combine, identity):
    length, mine = (lax.axis_size(axis), lax.axis_index(axis))
    everything = jax.tree.map(lambda part: lax.all_gather(part, axis), shard)
    start = jax.tree.map(
        lambda part, zero: jnp.broadcast_to(jnp.asarray(zero, part.dtype), part.shape),
        shard,
        identity,
    )

    def step(k, before):
        reached = k < mine
        new = combine(before, jax.tree.map(lambda part: part[k], everything))
        return jax.tree.map(lambda a, b: jnp.where(reached, a, b), new, before)

    return lax.fori_loop(0, length, step, start)


def passed_along_2(value, axis, steps):
    count = lax.axis_size(axis)
    leading, last = (max(0, -steps), min(count, count - steps))
    return lax.ppermute(value, axis, [(source, source + steps) for source in range(leading, last)])


def rms_rows(values):
    return values * lax.rsqrt(jnp.mean(values * values, axis=-1, keepdims=True) + EPSILON)


def rotary(values, position):
    half_count = values.shape[-1] // 2
    frequency = ROPE_BASE ** (-(jnp.arange(half_count, dtype=jnp.float32) * 2.0) / values.shape[-1])
    angles = position.astype(jnp.float32)[:, None] * frequency[None, :]
    cosine = jnp.concatenate([jnp.cos(angles), jnp.cos(angles)], axis=-1)[:, None, :]
    sine = jnp.concatenate([jnp.sin(angles), jnp.sin(angles)], axis=-1)[:, None, :]
    turned = jnp.concatenate([-values[..., half_count:], values[..., :half_count]], axis=-1)
    return values * cosine + turned * sine


def feed_forward(row_block, gate_part, up_part, down_part):
    gate_proj = jnp.dot(row_block, gate_part, preferred_element_type=jnp.float32)
    up_proj = jnp.dot(row_block, up_part, preferred_element_type=jnp.float32)
    activated = (jax.nn.silu(gate_proj) * up_proj).astype(jnp.bfloat16)
    return jnp.dot(activated, down_part, preferred_element_type=jnp.float32)


def keep_later(earlier, later):
    same_id = earlier[0] == later[0]
    newer_id = later[0] > earlier[0]
    start_at = jnp.where(
        same_id, jnp.minimum(earlier[1], later[1]), jnp.where(newer_id, later[1], earlier[1])
    )
    return (jnp.maximum(earlier[0], later[0]), start_at)


def on_device(
    tokens,
    routes,
    router_weights,
    w_gate,
    w_up,
    w_down,
    w_query,
    w_keyval,
    gain_query,
    gain_key,
    segment_ids,
):
    device_count = lax.axis_size(EP)
    expert_count = device_count // OWNERS
    token_count = tokens.shape[1]
    model_width = tokens.shape[2]
    capacity = OWNERS * max(1, token_count // device_count)
    wide_tokens = tokens[0].astype(jnp.float32)
    normed = rms_rows(wide_tokens).astype(jnp.bfloat16)
    inside = routes[0] < expert_count
    has_route = jnp.any(inside, axis=-1)
    chosen = jnp.sum(jnp.where(inside, routes[0], 0), axis=-1)
    weight_kept = jnp.sum(jnp.where(inside, router_weights[0], 0.0), axis=-1)
    expert_ids = jnp.arange(expert_count, dtype=jnp.int32)
    member = ((chosen[:, None] == expert_ids[None, :]) & has_route[:, None]).astype(jnp.int32)
    rank_within = jnp.sum((jnp.cumsum(member, axis=0) - member) * member, axis=-1)
    slot_index = jnp.where(has_route, chosen * capacity + rank_within, -1)
    slot_ids = jnp.arange(expert_count * capacity, dtype=jnp.int32)
    placing = (slot_ids[:, None] == slot_index[None, :]).astype(jnp.bfloat16)
    packed = jnp.dot(placing, normed, preferred_element_type=jnp.float32).astype(jnp.bfloat16)
    gate_part = w_gate[0, 0]
    up_part = w_up[0, 0]
    down_part = w_down[0, 0]
    spread = jnp.broadcast_to(
        packed.reshape(expert_count, 1, capacity, model_width),
        (expert_count, OWNERS, capacity, model_width),
    ).reshape(device_count, capacity, model_width)
    segment_row = segment_ids[0]
    first_index = lax.axis_index(EP) * token_count
    reach = (SEG_MOST - 1) // token_count + 1
    shard_rows = w_query.shape[1]
    per_row = -(-token_count // shard_rows)
    carried = jnp.pad(segment_row, (0, shard_rows * per_row - token_count)).reshape(
        shard_rows, per_row
    )
    carried = jnp.pad(carried.astype(jnp.bfloat16), ((0, 0), (0, 128 - per_row)))
    projection = jnp.concatenate([w_query[0], w_keyval[0], carried], axis=-1)
    projection = lax.all_gather(projection, EP[-1], axis=0, tiled=True)
    spread, projection = lax.optimization_barrier((spread, projection))
    projection = lax.all_gather(projection, EP[:-1], axis=0, tiled=True)
    received = lax.all_to_all(spread, EP, split_axis=0, concat_axis=0, tiled=True)
    partial_out = feed_forward(
        received.reshape(-1, model_width), gate_part, up_part, down_part
    ).reshape(received.shape)
    returned_rows = lax.all_to_all(
        partial_out.astype(jnp.bfloat16), EP, split_axis=0, concat_axis=0, tiled=True
    ).astype(partial_out.dtype)
    merged = jnp.sum(
        returned_rows.reshape(expert_count, OWNERS, capacity, model_width), axis=1
    ).reshape(expert_count * capacity, model_width)
    fetched_rows = jnp.take(merged, jnp.maximum(slot_index, 0), axis=0)
    expert_out = jnp.where(has_route[:, None], fetched_rows, 0.0)
    layer_out = (wide_tokens + weight_kept[:, None] * expert_out).astype(jnp.bfloat16)
    arrived = passed_along(layer_out, "section", 1)
    lifted = rms_rows(arrived.astype(jnp.float32)).astype(jnp.bfloat16)
    head_dim = gain_query.shape[-1]
    query_width = w_query.shape[-1]
    head_count = query_width // head_dim
    projected = jnp.dot(lifted, projection, preferred_element_type=jnp.float32)
    query_raw = projected[:, :query_width]
    keyval_raw = projected[:, query_width : query_width + 2 * head_dim]
    all_segments = (
        projection[:, query_width + 2 * head_dim :][:, :per_row]
        .astype(jnp.int32)
        .reshape(-1)[: device_count * token_count]
    )
    global_index = first_index + jnp.arange(token_count, dtype=jnp.int32)
    key_index = (
        first_index - reach * token_count + jnp.arange((reach + 1) * token_count, dtype=jnp.int32)
    )
    section_index = jnp.arange(device_count * token_count, dtype=jnp.int32)
    start_index = jnp.min(
        jnp.where(all_segments[None, :] == segment_row[:, None], section_index[None, :], FAR_INDEX),
        axis=1,
    )
    position = global_index - start_index
    query = rotary(
        rms_rows(query_raw.reshape(token_count, head_count, head_dim)) * gain_query[0], position
    ).astype(jnp.bfloat16)
    key_part = rotary(rms_rows(keyval_raw[:, None, :head_dim]) * gain_key[0], position)[
        :, 0
    ].astype(jnp.bfloat16)
    value_part = keyval_raw[:, head_dim:].astype(jnp.bfloat16)
    key_value = jnp.concatenate([key_part, value_part], axis=-1)
    earlier_pieces = []
    for distance in range(1, reach + 1):
        earlier_pieces.append(passed_along_2(key_value, EP, distance))
    window = jnp.concatenate(earlier_pieces[::-1] + [key_value], axis=0)
    score_scale = 1.0 / math.sqrt(head_dim)
    scores = (
        jnp.einsum(
            "thd,kd->thk", query, window[:, :head_dim], preferred_element_type=jnp.float32
        )
        * score_scale
    )
    allowed = (
        (key_index[None, :] >= start_index[:, None]) & (key_index[None, :] <= global_index[:, None])
    )[:, None, :]
    probabilities = jnp.where(allowed, jnp.exp(scores), 0.0)
    total_mass = jnp.sum(probabilities, axis=-1)
    mixed = jnp.einsum(
        "thk,kd->thd",
        probabilities.astype(jnp.bfloat16),
        window[:, head_dim:],
        preferred_element_type=jnp.float32,
    )
    attended = (mixed / total_mass[..., None]).astype(jnp.bfloat16).reshape(token_count, query_width)
    return (layer_out[None], attended[None])


def solution(mesh):
    ep_size = mesh.shape["ep"]
    z_size = 4 if ep_size % 4 == 0 else 1
    x_size = 4 if ep_size % (z_size * 4) == 0 else 1
    split_mesh = jax.sharding.Mesh(
        mesh.devices.reshape(
            mesh.shape["section"], ep_size // (x_size * z_size), x_size, z_size
        ),
        ("section",) + EP,
    )
    in_specs = (
        P("section", EP, None),
        P("section", EP, None),
        P("section", EP, None),
        P("section", EP, None, None),
        P("section", EP, None, None),
        P("section", EP, None, None),
        P("section", EP, None),
        P("section", EP, None),
        P("section", None),
        P("section", None),
        P("section", EP),
    )
    out_specs = (P("section", EP, None), P("section", EP, None))
    return jax.shard_map(
        on_device, mesh=split_mesh, in_specs=in_specs, out_specs=out_specs, check_vma=False
    )
```

```python
import math

import jax
import jax.numpy as jnp
from jax import lax
from jax.sharding import PartitionSpec as P

OWNERS = 4
SEG_MOST = 512


EPSILON = 1e-06
ROPE_BASE = 1000000.0
FAR_INDEX = 1073741824
EP = ("ep_y", "ep_x", "ep_z")


def passed_along(block, axis, distance):
    devices = range(lax.axis_size(axis))
    route = [((i - distance) % len(devices), i) for i in devices]
    return lax.ppermute(block, axis, route)


def prefix(shard, axis, combine, identity):
    length, mine = (lax.axis_size(axis), lax.axis_index(axis))
    everything = jax.tree.map(lambda part: lax.all_gather(part, axis), shard)
    start = jax.tree.map(
        lambda part, zero: jnp.broadcast_to(jnp.asarray(zero, part.dtype), part.shape),
        shard,
        identity,
    )

    def step(k, before):
        reached = k < mine
        new = combine(before, jax.tree.map(lambda part: part[k], everything))
        return jax.tree.map(lambda a, b: jnp.where(reached, a, b), new, before)

    return lax.fori_loop(0, length, step, start)


def passed_along_2(value, axis, steps):
    count = lax.axis_size(axis)
    leading, last = (max(0, -steps), min(count, count - steps))
    return lax.ppermute(value, axis, [(source, source + steps) for source in range(leading, last)])


def rms_rows(values):
    return values * lax.rsqrt(jnp.mean(values * values, axis=-1, keepdims=True) + EPSILON)


def rotary(values, position):
    half_count = values.shape[-1] // 2
    frequency = ROPE_BASE ** (-(jnp.arange(half_count, dtype=jnp.float32) * 2.0) / values.shape[-1])
    angles = position.astype(jnp.float32)[:, None] * frequency[None, :]
    cosine = jnp.concatenate([jnp.cos(angles), jnp.cos(angles)], axis=-1)[:, None, :]
    sine = jnp.concatenate([jnp.sin(angles), jnp.sin(angles)], axis=-1)[:, None, :]
    turned = jnp.concatenate([-values[..., half_count:], values[..., :half_count]], axis=-1)
    return values * cosine + turned * sine


def feed_forward(row_block, gate_part, up_part, down_part):
    gate_proj = jnp.dot(row_block, gate_part, preferred_element_type=jnp.float32)
    up_proj = jnp.dot(row_block, up_part, preferred_element_type=jnp.float32)
    activated = (jax.nn.silu(gate_proj) * up_proj).astype(jnp.bfloat16)
    return jnp.dot(activated, down_part, preferred_element_type=jnp.float32)


def keep_later(earlier, later):
    same_id = earlier[0] == later[0]
    newer_id = later[0] > earlier[0]
    start_at = jnp.where(
        same_id, jnp.minimum(earlier[1], later[1]), jnp.where(newer_id, later[1], earlier[1])
    )
    return (jnp.maximum(earlier[0], later[0]), start_at)


def on_device(
    tokens,
    routes,
    router_weights,
    w_gate,
    w_up,
    w_down,
    w_query,
    w_keyval,
    gain_query,
    gain_key,
    segment_ids,
):
    device_count = lax.axis_size(EP)
    expert_count = device_count // OWNERS
    token_count = tokens.shape[1]
    model_width = tokens.shape[2]
    capacity = OWNERS * max(1, token_count // device_count)
    wide_tokens = tokens[0].astype(jnp.float32)
    normed = rms_rows(wide_tokens).astype(jnp.bfloat16)
    inside = routes[0] < expert_count
    has_route = jnp.any(inside, axis=-1)
    chosen = jnp.sum(jnp.where(inside, routes[0], 0), axis=-1)
    weight_kept = jnp.sum(jnp.where(inside, router_weights[0], 0.0), axis=-1)
    expert_ids = jnp.arange(expert_count, dtype=jnp.int32)
    member = ((chosen[:, None] == expert_ids[None, :]) & has_route[:, None]).astype(jnp.int32)
    rank_within = jnp.sum((jnp.cumsum(member, axis=0) - member) * member, axis=-1)
    slot_index = jnp.where(has_route, chosen * capacity + rank_within, -1)
    slot_ids = jnp.arange(expert_count * capacity, dtype=jnp.int32)
    placing = (slot_ids[:, None] == slot_index[None, :]).astype(jnp.bfloat16)
    packed = jnp.dot(placing, normed, preferred_element_type=jnp.float32).astype(jnp.bfloat16)
    gate_part = w_gate[0, 0]
    up_part = w_up[0, 0]
    down_part = w_down[0, 0]
    spread = jnp.broadcast_to(
        packed.reshape(expert_count, 1, capacity, model_width),
        (expert_count, OWNERS, capacity, model_width),
    ).reshape(device_count, capacity, model_width)
    next_query, next_keyval, segment_row, next_gain_query, next_gain_key = passed_along(
        (w_query[0], w_keyval[0], segment_ids[0], gain_query[0], gain_key[0]), "section", -1
    )
    first_index = lax.axis_index(EP) * token_count
    reach = (SEG_MOST - 1) // token_count + 1
    shard_rows = next_query.shape[0]
    per_row = -(-token_count // shard_rows)
    carried = jnp.pad(segment_row, (0, shard_rows * per_row - token_count)).reshape(
        shard_rows, per_row
    )
    carried = jnp.pad(carried.astype(jnp.bfloat16), ((0, 0), (0, 128 - per_row)))
    projection = jnp.concatenate([next_query, next_keyval, carried], axis=-1)
    projection = lax.all_gather(projection, EP[1:], axis=0, tiled=True)
    projection = lax.all_gather(projection, EP[:1], axis=0, tiled=True)
    received = lax.all_to_all(spread, EP, split_axis=0, concat_axis=0, tiled=True)
    partial_out = feed_forward(
        received.reshape(-1, model_width), gate_part, up_part, down_part
    ).reshape(received.shape)
    returned_rows = lax.all_to_all(
        partial_out.astype(jnp.bfloat16), EP, split_axis=0, concat_axis=0, tiled=True
    ).astype(partial_out.dtype)
    merged = jnp.sum(
        returned_rows.reshape(expert_count, OWNERS, capacity, model_width), axis=1
    ).reshape(expert_count * capacity, model_width)
    fetched_rows = jnp.take(merged, jnp.maximum(slot_index, 0), axis=0)
    expert_out = jnp.where(has_route[:, None], fetched_rows, 0.0)
    layer_out = (wide_tokens + weight_kept[:, None] * expert_out).astype(jnp.bfloat16)
    lifted = rms_rows(layer_out.astype(jnp.float32)).astype(jnp.bfloat16)
    head_dim = gain_query.shape[-1]
    query_width = w_query.shape[-1]
    head_count = query_width // head_dim
    projected = jnp.dot(lifted, projection, preferred_element_type=jnp.float32)
    query_raw = projected[:, :query_width]
    keyval_raw = projected[:, query_width : query_width + 2 * head_dim]
    all_segments = (
        projection[:, query_width + 2 * head_dim :][:, :per_row]
        .astype(jnp.int32)
        .reshape(-1)[: device_count * token_count]
    )
    global_index = first_index + jnp.arange(token_count, dtype=jnp.int32)
    key_index = (
        first_index - reach * token_count + jnp.arange((reach + 1) * token_count, dtype=jnp.int32)
    )
    section_index = jnp.arange(device_count * token_count, dtype=jnp.int32)
    start_index = jnp.min(
        jnp.where(all_segments[None, :] == segment_row[:, None], section_index[None, :], FAR_INDEX),
        axis=1,
    )
    position = global_index - start_index
    query = rotary(
        rms_rows(query_raw.reshape(token_count, head_count, head_dim)) * next_gain_query, position
    ).astype(jnp.bfloat16)
    key_part = rotary(rms_rows(keyval_raw[:, None, :head_dim]) * next_gain_key, position)[
        :, 0
    ].astype(jnp.bfloat16)
    value_part = keyval_raw[:, head_dim:].astype(jnp.bfloat16)
    key_value = jnp.concatenate([key_part, value_part], axis=-1)
    earlier_pieces = []
    for distance in range(1, reach + 1):
        earlier_pieces.append(passed_along_2(key_value, EP, distance))
    window = jnp.concatenate(earlier_pieces[::-1] + [key_value], axis=0)
    score_scale = 1.0 / math.sqrt(head_dim)
    scores = (
        jnp.einsum(
            "thd,kd->thk", query, window[:, :head_dim], preferred_element_type=jnp.float32
        )
        * score_scale
    )
    allowed = (
        (key_index[None, :] >= start_index[:, None]) & (key_index[None, :] <= global_index[:, None])
    )[:, None, :]
    probabilities = jnp.where(allowed, jnp.exp(scores), 0.0)
    total_mass = jnp.sum(probabilities, axis=-1)
    mixed = jnp.einsum(
        "thk,kd->thd",
        probabilities.astype(jnp.bfloat16),
        window[:, head_dim:],
        preferred_element_type=jnp.float32,
    )
    attended = (mixed / total_mass[..., None]).astype(jnp.bfloat16).reshape(token_count, query_width)
    attended = passed_along(attended, "section", 1)
    return (layer_out[None], attended[None])


def solution(mesh):
    ep_size = mesh.shape["ep"]
    z_size = 4 if ep_size % 4 == 0 else 1
    x_size = 4 if ep_size % (z_size * 4) == 0 else 1
    split_mesh = jax.sharding.Mesh(
        mesh.devices.reshape(
            mesh.shape["section"], ep_size // (x_size * z_size), x_size, z_size
        ),
        ("section",) + EP,
    )
    in_specs = (
        P("section", EP, None),
        P("section", EP, None),
        P("section", EP, None),
        P("section", EP, None, None),
        P("section", EP, None, None),
        P("section", EP, None, None),
        P("section", EP, None),
        P("section", EP, None),
        P("section", None),
        P("section", None),
        P("section", EP),
    )
    out_specs = (P("section", EP, None), P("section", EP, None))
    return jax.shard_map(
        on_device, mesh=split_mesh, in_specs=in_specs, out_specs=out_specs, check_vma=False
    )
```

```python
import math

import jax
import jax.numpy as jnp
from jax import lax
from jax.sharding import PartitionSpec as P

OWNERS = 4
SEG_MOST = 512


EPSILON = 1e-06
ROPE_BASE = 1000000.0
FAR_INDEX = 1073741824
EP = ("ep_y", "ep_x", "ep_z")


def passed_along(block, axis, distance):
    devices = range(lax.axis_size(axis))
    route = [((i - distance) % len(devices), i) for i in devices]
    return lax.ppermute(block, axis, route)


def prefix(shard, axis, combine, identity):
    length, mine = (lax.axis_size(axis), lax.axis_index(axis))
    everything = jax.tree.map(lambda part: lax.all_gather(part, axis), shard)
    start = jax.tree.map(
        lambda part, zero: jnp.broadcast_to(jnp.asarray(zero, part.dtype), part.shape),
        shard,
        identity,
    )

    def step(k, before):
        reached = k < mine
        new = combine(before, jax.tree.map(lambda part: part[k], everything))
        return jax.tree.map(lambda a, b: jnp.where(reached, a, b), new, before)

    return lax.fori_loop(0, length, step, start)


def passed_along_2(value, axis, steps):
    count = lax.axis_size(axis)
    leading, last = (max(0, -steps), min(count, count - steps))
    return lax.ppermute(value, axis, [(source, source + steps) for source in range(leading, last)])


def rms_rows(values):
    return values * lax.rsqrt(jnp.mean(values * values, axis=-1, keepdims=True) + EPSILON)


def rotary(values, position):
    half_count = values.shape[-1] // 2
    frequency = ROPE_BASE ** (-(jnp.arange(half_count, dtype=jnp.float32) * 2.0) / values.shape[-1])
    angles = position.astype(jnp.float32)[:, None] * frequency[None, :]
    cosine = jnp.concatenate([jnp.cos(angles), jnp.cos(angles)], axis=-1)[:, None, :]
    sine = jnp.concatenate([jnp.sin(angles), jnp.sin(angles)], axis=-1)[:, None, :]
    turned = jnp.concatenate([-values[..., half_count:], values[..., :half_count]], axis=-1)
    return values * cosine + turned * sine


def feed_forward(row_block, gate_part, up_part, down_part):
    gate_proj = jnp.dot(row_block, gate_part, preferred_element_type=jnp.float32)
    up_proj = jnp.dot(row_block, up_part, preferred_element_type=jnp.float32)
    activated = (jax.nn.silu(gate_proj) * up_proj).astype(jnp.bfloat16)
    return jnp.dot(activated, down_part, preferred_element_type=jnp.float32)


def keep_later(earlier, later):
    same_id = earlier[0] == later[0]
    newer_id = later[0] > earlier[0]
    start_at = jnp.where(
        same_id, jnp.minimum(earlier[1], later[1]), jnp.where(newer_id, later[1], earlier[1])
    )
    return (jnp.maximum(earlier[0], later[0]), start_at)


def on_device(
    tokens,
    routes,
    router_weights,
    w_gate,
    w_up,
    w_down,
    w_query,
    w_keyval,
    gain_query,
    gain_key,
    segment_ids,
):
    device_count = lax.axis_size(EP)
    expert_count = device_count // OWNERS
    token_count = tokens.shape[1]
    model_width = tokens.shape[2]
    capacity = OWNERS * max(1, token_count // device_count)
    wide_tokens = tokens[0].astype(jnp.float32)
    normed = rms_rows(wide_tokens).astype(jnp.bfloat16)
    inside = routes[0] < expert_count
    has_route = jnp.any(inside, axis=-1)
    chosen = jnp.sum(jnp.where(inside, routes[0], 0), axis=-1)
    weight_kept = jnp.sum(jnp.where(inside, router_weights[0], 0.0), axis=-1)
    expert_ids = jnp.arange(expert_count, dtype=jnp.int32)
    member = ((chosen[:, None] == expert_ids[None, :]) & has_route[:, None]).astype(jnp.int32)
    rank_within = jnp.sum((jnp.cumsum(member, axis=0) - member) * member, axis=-1)
    slot_index = jnp.where(has_route, chosen * capacity + rank_within, -1)
    slot_ids = jnp.arange(expert_count * capacity, dtype=jnp.int32)
    placing = (slot_ids[:, None] == slot_index[None, :]).astype(jnp.bfloat16)
    packed = jnp.dot(placing, normed, preferred_element_type=jnp.float32).astype(jnp.bfloat16)
    gate_part = w_gate[0, 0]
    up_part = w_up[0, 0]
    down_part = w_down[0, 0]
    spread = jnp.broadcast_to(
        packed.reshape(expert_count, 1, capacity, model_width),
        (expert_count, OWNERS, capacity, model_width),
    ).reshape(device_count, capacity, model_width)
    next_query, next_keyval, segment_row, next_gain_query, next_gain_key = passed_along(
        (w_query[0], w_keyval[0], segment_ids[0], gain_query[0], gain_key[0]), "section", -1
    )
    first_index = lax.axis_index(EP) * token_count
    reach = (SEG_MOST - 1) // token_count + 1
    shard_rows = next_query.shape[0]
    per_row = -(-token_count // shard_rows)
    carried = jnp.pad(segment_row, (0, shard_rows * per_row - token_count)).reshape(
        shard_rows, per_row
    )
    carried = jnp.pad(carried.astype(jnp.bfloat16), ((0, 0), (0, 128 - per_row)))
    projection = jnp.concatenate([next_query, next_keyval, carried], axis=-1)
    projection = lax.all_gather(projection, EP[-1], axis=0, tiled=True)
    spread, projection = lax.optimization_barrier((spread, projection))
    projection = lax.all_gather(projection, EP[:-1], axis=0, tiled=True)
    received = lax.all_to_all(spread, EP, split_axis=0, concat_axis=0, tiled=True)
    partial_out = feed_forward(
        received.reshape(-1, model_width), gate_part, up_part, down_part
    ).reshape(received.shape)
    returned_rows = lax.all_to_all(
        partial_out.astype(jnp.bfloat16), EP, split_axis=0, concat_axis=0, tiled=True
    ).astype(partial_out.dtype)
    merged = jnp.sum(
        returned_rows.reshape(expert_count, OWNERS, capacity, model_width), axis=1
    ).reshape(expert_count * capacity, model_width)
    fetched_rows = jnp.take(merged, jnp.maximum(slot_index, 0), axis=0)
    expert_out = jnp.where(has_route[:, None], fetched_rows, 0.0)
    layer_out = (wide_tokens + weight_kept[:, None] * expert_out).astype(jnp.bfloat16)
    lifted = rms_rows(layer_out.astype(jnp.float32)).astype(jnp.bfloat16)
    head_dim = gain_query.shape[-1]
    query_width = w_query.shape[-1]
    head_count = query_width // head_dim
    projected = jnp.dot(lifted, projection, preferred_element_type=jnp.float32)
    query_raw = projected[:, :query_width]
    keyval_raw = projected[:, query_width : query_width + 2 * head_dim]
    all_segments = (
        projection[:, query_width + 2 * head_dim :][:, :per_row]
        .astype(jnp.int32)
        .reshape(-1)[: device_count * token_count]
    )
    global_index = first_index + jnp.arange(token_count, dtype=jnp.int32)
    key_index = (
        first_index - reach * token_count + jnp.arange((reach + 1) * token_count, dtype=jnp.int32)
    )
    section_index = jnp.arange(device_count * token_count, dtype=jnp.int32)
    start_index = jnp.min(
        jnp.where(all_segments[None, :] == segment_row[:, None], section_index[None, :], FAR_INDEX),
        axis=1,
    )
    position = global_index - start_index
    query = rotary(
        rms_rows(query_raw.reshape(token_count, head_count, head_dim)) * next_gain_query, position
    ).astype(jnp.bfloat16)
    key_part = rotary(rms_rows(keyval_raw[:, None, :head_dim]) * next_gain_key, position)[
        :, 0
    ].astype(jnp.bfloat16)
    value_part = keyval_raw[:, head_dim:].astype(jnp.bfloat16)
    key_value = jnp.concatenate([key_part, value_part], axis=-1)
    earlier_pieces = []
    for distance in range(1, reach + 1):
        earlier_pieces.append(passed_along_2(key_value, EP, distance))
    window = jnp.concatenate(earlier_pieces[::-1] + [key_value], axis=0)
    score_scale = 1.0 / math.sqrt(head_dim)
    scores = (
        jnp.einsum(
            "thd,kd->thk", query, window[:, :head_dim], preferred_element_type=jnp.float32
        )
        * score_scale
    )
    allowed = (
        (key_index[None, :] >= start_index[:, None]) & (key_index[None, :] <= global_index[:, None])
    )[:, None, :]
    probabilities = jnp.where(allowed, jnp.exp(scores), 0.0)
    total_mass = jnp.sum(probabilities, axis=-1)
    mixed = jnp.einsum(
        "thk,kd->thd",
        probabilities.astype(jnp.bfloat16),
        window[:, head_dim:],
        preferred_element_type=jnp.float32,
    )
    attended = (mixed / total_mass[..., None]).astype(jnp.bfloat16).reshape(token_count, query_width)
    attended = passed_along(attended, "section", 1)
    return (layer_out[None], attended[None])


def solution(mesh):
    ep_size = mesh.shape["ep"]
    z_size = 4 if ep_size % 4 == 0 else 1
    x_size = 4 if ep_size % (z_size * 4) == 0 else 1
    split_mesh = jax.sharding.Mesh(
        mesh.devices.reshape(
            mesh.shape["section"], ep_size // (x_size * z_size), x_size, z_size
        ),
        ("section",) + EP,
    )
    in_specs = (
        P("section", EP, None),
        P("section", EP, None),
        P("section", EP, None),
        P("section", EP, None, None),
        P("section", EP, None, None),
        P("section", EP, None, None),
        P("section", EP, None),
        P("section", EP, None),
        P("section", None),
        P("section", None),
        P("section", EP),
    )
    out_specs = (P("section", EP, None), P("section", EP, None))
    return jax.shard_map(
        on_device, mesh=split_mesh, in_specs=in_specs, out_specs=out_specs, check_vma=False
    )
```

```python
import math

import jax
import jax.numpy as jnp
from jax import lax
from jax.sharding import PartitionSpec as P


OWNERS = 4
SEG_MOST = 512


EPSILON = 1e-06
ROPE_BASE = 1000000.0
FAR_INDEX = 1073741824
EP = ("ep_y", "ep_x", "ep_z")


def passed_along(block, axis, distance):
    devices = range(lax.axis_size(axis))
    route = [((i - distance) % len(devices), i) for i in devices]
    return lax.ppermute(block, axis, route)


def passed_along_2(value, axis, steps):
    count = lax.axis_size(axis)
    leading, last = (max(0, -steps), min(count, count - steps))
    return lax.ppermute(value, axis, [(source, source + steps) for source in range(leading, last)])


def rms_rows(values):
    return values * lax.rsqrt(jnp.mean(values * values, axis=-1, keepdims=True) + EPSILON)


def rotary(values, position):
    half_count = values.shape[-1] // 2
    frequency = ROPE_BASE ** (-(jnp.arange(half_count, dtype=jnp.float32) * 2.0) / values.shape[-1])
    angles = position.astype(jnp.float32)[:, None] * frequency[None, :]
    cosine = jnp.concatenate([jnp.cos(angles), jnp.cos(angles)], axis=-1)[:, None, :]
    sine = jnp.concatenate([jnp.sin(angles), jnp.sin(angles)], axis=-1)[:, None, :]
    turned = jnp.concatenate([-values[..., half_count:], values[..., :half_count]], axis=-1)
    return values * cosine + turned * sine


def feed_forward(row_block, gate_part, up_part, down_part):
    gate_proj = jnp.dot(row_block, gate_part, preferred_element_type=jnp.float32)
    up_proj = jnp.dot(row_block, up_part, preferred_element_type=jnp.float32)
    activated = (jax.nn.silu(gate_proj) * up_proj).astype(jnp.bfloat16)
    return jnp.dot(activated, down_part, preferred_element_type=jnp.float32)


def on_device(
    tokens,
    routes,
    router_weights,
    w_gate,
    w_up,
    w_down,
    w_query,
    w_keyval,
    gain_query,
    gain_key,
    segment_ids,
):
    device_count = lax.axis_size(EP)
    expert_count = device_count // OWNERS
    token_count = tokens.shape[1]
    model_width = tokens.shape[2]
    capacity = OWNERS * max(1, token_count // device_count)
    wide_tokens = tokens[0].astype(jnp.float32)
    normed = rms_rows(wide_tokens).astype(jnp.bfloat16)
    inside = routes[0] < expert_count
    has_route = jnp.any(inside, axis=-1)
    chosen = jnp.sum(jnp.where(inside, routes[0], 0), axis=-1)
    weight_kept = jnp.sum(jnp.where(inside, router_weights[0], 0.0), axis=-1)
    expert_ids = jnp.arange(expert_count, dtype=jnp.int32)
    member = ((chosen[:, None] == expert_ids[None, :]) & has_route[:, None]).astype(jnp.int32)
    rank_within = jnp.sum((jnp.cumsum(member, axis=0) - member) * member, axis=-1)
    slot_index = jnp.where(has_route, chosen * capacity + rank_within, -1)
    slot_ids = jnp.arange(expert_count * capacity, dtype=jnp.int32)
    placing = (slot_ids[:, None] == slot_index[None, :]).astype(jnp.bfloat16)
    packed = jnp.dot(placing, normed, preferred_element_type=jnp.float32).astype(jnp.bfloat16)
    gate_part = w_gate[0, 0]
    up_part = w_up[0, 0]
    down_part = w_down[0, 0]
    spread = jnp.broadcast_to(
        packed.reshape(expert_count, 1, capacity, model_width),
        (expert_count, OWNERS, capacity, model_width),
    ).reshape(device_count, capacity, model_width)
    next_query, next_keyval, segment_row, next_gain_query, next_gain_key = passed_along(
        (w_query[0], w_keyval[0], segment_ids[0], gain_query[0], gain_key[0]), "section", -1
    )
    first_index = lax.axis_index(EP) * token_count
    reach = (SEG_MOST - 1) // token_count + 1
    shard_rows = next_query.shape[0]
    per_row = -(-token_count // shard_rows)
    carried = jnp.pad(segment_row, (0, shard_rows * per_row - token_count)).reshape(
        shard_rows, per_row
    )
    carried = jnp.pad(carried.astype(jnp.bfloat16), ((0, 0), (0, 128 - per_row)))
    projection = jnp.concatenate([next_query, next_keyval, carried], axis=-1)
    projection = lax.all_gather(projection, EP[-1], axis=0, tiled=True)
    spread, projection = lax.optimization_barrier((spread, projection))
    projection = lax.all_gather(projection, EP[:-1], axis=0, tiled=True)
    received = lax.all_to_all(spread, EP, split_axis=0, concat_axis=0, tiled=True)
    partial_out = feed_forward(
        received.reshape(-1, model_width), gate_part, up_part, down_part
    ).reshape(received.shape)
    returned_rows = lax.all_to_all(
        partial_out.astype(jnp.bfloat16), EP, split_axis=0, concat_axis=0, tiled=True
    )
    returned_rows = returned_rows.astype(partial_out.dtype)
    merged = jnp.sum(
        returned_rows.reshape(expert_count, OWNERS, capacity, model_width), axis=1
    ).reshape(expert_count * capacity, model_width)
    fetched_rows = jnp.take(merged, jnp.maximum(slot_index, 0), axis=0)
    expert_out = jnp.where(has_route[:, None], fetched_rows, 0.0)
    layer_out = (wide_tokens + weight_kept[:, None] * expert_out).astype(jnp.bfloat16)
    lifted = rms_rows(layer_out.astype(jnp.float32)).astype(jnp.bfloat16)
    head_dim = gain_query.shape[-1]
    query_width = w_query.shape[-1]
    head_count = query_width // head_dim
    projected = jnp.dot(lifted, projection, preferred_element_type=jnp.float32)
    query_raw = projected[:, :query_width]
    keyval_raw = projected[:, query_width : query_width + 2 * head_dim]
    all_segments = (
        projection[:, query_width + 2 * head_dim :][:, :per_row]
        .astype(jnp.int32)
        .reshape(-1)[: device_count * token_count]
    )
    global_index = first_index + jnp.arange(token_count, dtype=jnp.int32)
    section_index = jnp.arange(device_count * token_count, dtype=jnp.int32)
    start_index = jnp.min(
        jnp.where(all_segments[None, :] == segment_row[:, None], section_index[None, :], FAR_INDEX),
        axis=1,
    )
    position = global_index - start_index
    key_index = (
        first_index - reach * token_count + jnp.arange((reach + 1) * token_count, dtype=jnp.int32)
    )
    query = rotary(
        rms_rows(query_raw.reshape(token_count, head_count, head_dim)) * next_gain_query, position
    ).astype(jnp.bfloat16)
    key_part = rotary(rms_rows(keyval_raw[:, None, :head_dim]) * next_gain_key, position)[
        :, 0
    ].astype(jnp.bfloat16)
    value_part = keyval_raw[:, head_dim:].astype(jnp.bfloat16)
    key_value = jnp.concatenate([key_part, value_part], axis=-1)
    earlier_pieces = []
    for distance in range(1, reach + 1):
        earlier_pieces.append(passed_along_2(key_value, EP, distance))
    window = jnp.concatenate(earlier_pieces[::-1] + [key_value], axis=0)
    score_scale = 1.0 / math.sqrt(head_dim)
    scores = (
        jnp.einsum(
            "thd,kd->thk", query, window[:, :head_dim], preferred_element_type=jnp.float32
        )
        * score_scale
    )
    allowed = (
        (key_index[None, :] >= start_index[:, None]) & (key_index[None, :] <= global_index[:, None])
    )[:, None, :]
    probabilities = jnp.where(allowed, jnp.exp(scores), 0.0)
    total_mass = jnp.sum(probabilities, axis=-1)
    mixed = jnp.einsum(
        "thk,kd->thd",
        probabilities.astype(jnp.bfloat16),
        window[:, head_dim:],
        preferred_element_type=jnp.float32,
    )
    attended = (mixed / total_mass[..., None]).astype(jnp.bfloat16).reshape(token_count, query_width)
    attended = passed_along(attended, "section", 1)
    return (layer_out[None], attended[None])


def solution(mesh):
    ep_size = mesh.shape["ep"]
    z_size = 4 if ep_size % 4 == 0 else 1
    x_size = 4 if ep_size % (z_size * 4) == 0 else 1
    split_mesh = jax.sharding.Mesh(
        mesh.devices.reshape(
            mesh.shape["section"], ep_size // (x_size * z_size), x_size, z_size
        ),
        ("section",) + EP,
    )
    in_specs = (
        P("section", EP, None),
        P("section", EP, None),
        P("section", EP, None),
        P("section", EP, None, None),
        P("section", EP, None, None),
        P("section", EP, None, None),
        P("section", EP, None),
        P("section", EP, None),
        P("section", None),
        P("section", None),
        P("section", EP),
    )
    out_specs = (P("section", EP, None), P("section", EP, None))

    return jax.shard_map(
        on_device, mesh=split_mesh, in_specs=in_specs, out_specs=out_specs, check_vma=False
    )
```

```python
import math

import jax
import jax.numpy as jnp
from jax import lax
from jax.sharding import PartitionSpec as P


OWNERS = 4
SEG_MOST = 512


EPSILON = 1e-06
ROPE_BASE = 1000000.0
FAR_INDEX = 1073741824
EP = ("ep_y", "ep_x", "ep_z")


def passed_along(block, axis, distance):
    devices = range(lax.axis_size(axis))
    route = [((i - distance) % len(devices), i) for i in devices]
    return lax.ppermute(block, axis, route)


def passed_along_2(value, axis, steps):
    count = lax.axis_size(axis)
    leading, last = (max(0, -steps), min(count, count - steps))
    return lax.ppermute(value, axis, [(source, source + steps) for source in range(leading, last)])


def rms_rows(values):
    return values * lax.rsqrt(jnp.mean(values * values, axis=-1, keepdims=True) + EPSILON)


def rotary(values, position):
    half_count = values.shape[-1] // 2
    frequency = ROPE_BASE ** (-(jnp.arange(half_count, dtype=jnp.float32) * 2.0) / values.shape[-1])
    angles = position.astype(jnp.float32)[:, None] * frequency[None, :]
    cosine = jnp.concatenate([jnp.cos(angles), jnp.cos(angles)], axis=-1)[:, None, :]
    sine = jnp.concatenate([jnp.sin(angles), jnp.sin(angles)], axis=-1)[:, None, :]
    turned = jnp.concatenate([-values[..., half_count:], values[..., :half_count]], axis=-1)
    return values * cosine + turned * sine


def feed_forward(row_block, gate_part, up_part, down_part):
    gate_proj = jnp.dot(row_block, gate_part, preferred_element_type=jnp.float32)
    up_proj = jnp.dot(row_block, up_part, preferred_element_type=jnp.float32)
    activated = (jax.nn.silu(gate_proj) * up_proj).astype(jnp.bfloat16)
    return jnp.dot(activated, down_part, preferred_element_type=jnp.float32)


def on_device(
    tokens,
    routes,
    router_weights,
    w_gate,
    w_up,
    w_down,
    w_query,
    w_keyval,
    gain_query,
    gain_key,
    segment_ids,
):
    device_count = lax.axis_size(EP)
    expert_count = device_count // OWNERS
    token_count = tokens.shape[1]
    model_width = tokens.shape[2]
    capacity = OWNERS * max(1, token_count // device_count)
    wide_tokens = tokens[0].astype(jnp.float32)
    normed = rms_rows(wide_tokens).astype(jnp.bfloat16)
    inside = routes[0] < expert_count
    has_route = jnp.any(inside, axis=-1)
    chosen = jnp.sum(jnp.where(inside, routes[0], 0), axis=-1)
    weight_kept = jnp.sum(jnp.where(inside, router_weights[0], 0.0), axis=-1)
    expert_ids = jnp.arange(expert_count, dtype=jnp.int32)
    member = ((chosen[:, None] == expert_ids[None, :]) & has_route[:, None]).astype(jnp.int32)
    rank_within = jnp.sum((jnp.cumsum(member, axis=0) - member) * member, axis=-1)
    slot_index = jnp.where(has_route, chosen * capacity + rank_within, -1)
    row_ids = jnp.arange(device_count * capacity, dtype=jnp.int32)
    row_expert = row_ids // (OWNERS * capacity)
    row_slot = row_ids % capacity
    placing = (
        (row_expert * capacity + row_slot)[:, None] == slot_index[None, :]
    ).astype(jnp.bfloat16)
    spread = (
        jnp.dot(placing, normed, preferred_element_type=jnp.float32)
        .astype(jnp.bfloat16)
        .reshape(device_count, capacity, model_width)
    )
    gate_part = w_gate[0, 0]
    up_part = w_up[0, 0]
    down_part = w_down[0, 0]
    segment_row, next_gain_query, next_gain_key = passed_along(
        (segment_ids[0], gain_query[0], gain_key[0]), "section", -1
    )
    first_index = lax.axis_index(EP) * token_count
    reach = (SEG_MOST - 1) // token_count + 1
    shard_rows = w_query.shape[1]
    per_row = -(-token_count // shard_rows)
    carried = jnp.pad(segment_ids[0], (0, shard_rows * per_row - token_count)).reshape(
        shard_rows, per_row
    )
    carried = jnp.pad(carried.astype(jnp.bfloat16), ((0, 0), (0, 128 - per_row)))
    own_shard = jnp.concatenate([w_query[0], w_keyval[0], carried], axis=-1)
    section_count = lax.axis_size("section")
    owner_count = lax.axis_size(EP[-1])
    pieces = []
    for shift in range(owner_count):
        route = [
            (((s + 1) % section_count) * owner_count + (z + shift) % owner_count, s * owner_count + z)
            for s in range(section_count)
            for z in range(owner_count)
        ]
        pieces.append(lax.ppermute(own_shard, ("section", EP[-1]), route))
    projection = jnp.roll(jnp.stack(pieces), lax.axis_index(EP[-1]), axis=0)
    projection = projection.reshape(-1, own_shard.shape[-1])
    spread, projection = lax.optimization_barrier((spread, projection))
    projection = lax.all_gather(projection, EP[:-1], axis=0, tiled=True)
    received = lax.all_to_all(spread, EP, split_axis=0, concat_axis=0, tiled=True)
    partial_out = feed_forward(
        received.reshape(-1, model_width), gate_part, up_part, down_part
    ).reshape(received.shape)
    returned_rows = lax.all_to_all(
        partial_out.astype(jnp.bfloat16), EP, split_axis=0, concat_axis=0, tiled=True
    )
    expert_out = jnp.dot(
        placing.T, returned_rows.reshape(-1, model_width), preferred_element_type=jnp.float32
    )
    layer_out = (wide_tokens + weight_kept[:, None] * expert_out).astype(jnp.bfloat16)
    lifted = rms_rows(layer_out.astype(jnp.float32)).astype(jnp.bfloat16)
    head_dim = gain_query.shape[-1]
    query_width = w_query.shape[-1]
    head_count = query_width // head_dim
    projected = jnp.dot(lifted, projection, preferred_element_type=jnp.float32)
    query_raw = projected[:, :query_width]
    keyval_raw = projected[:, query_width : query_width + 2 * head_dim]
    all_segments = (
        projection[:, query_width + 2 * head_dim :][:, :per_row]
        .astype(jnp.int32)
        .reshape(-1)[: device_count * token_count]
    )
    global_index = first_index + jnp.arange(token_count, dtype=jnp.int32)
    section_index = jnp.arange(device_count * token_count, dtype=jnp.int32)
    start_index = jnp.min(
        jnp.where(all_segments[None, :] == segment_row[:, None], section_index[None, :], FAR_INDEX),
        axis=1,
    )
    position = global_index - start_index
    key_index = (
        first_index - reach * token_count + jnp.arange((reach + 1) * token_count, dtype=jnp.int32)
    )
    query = rotary(
        rms_rows(query_raw.reshape(token_count, head_count, head_dim)) * next_gain_query, position
    ).astype(jnp.bfloat16)
    key_part = rotary(rms_rows(keyval_raw[:, None, :head_dim]) * next_gain_key, position)[
        :, 0
    ].astype(jnp.bfloat16)
    value_part = keyval_raw[:, head_dim:].astype(jnp.bfloat16)
    key_value = jnp.concatenate([key_part, value_part], axis=-1)
    earlier_pieces = []
    for distance in range(1, reach + 1):
        earlier_pieces.append(passed_along_2(key_value, EP, distance))
    window = jnp.concatenate(earlier_pieces[::-1] + [key_value], axis=0)
    score_scale = 1.0 / math.sqrt(head_dim)
    scores = (
        jnp.einsum(
            "thd,kd->thk", query, window[:, :head_dim], preferred_element_type=jnp.float32
        )
        * score_scale
    )
    allowed = (
        (key_index[None, :] >= start_index[:, None]) & (key_index[None, :] <= global_index[:, None])
    )[:, None, :]
    probabilities = jnp.where(allowed, jnp.exp(scores), 0.0)
    total_mass = jnp.sum(probabilities, axis=-1)
    mixed = jnp.einsum(
        "thk,kd->thd",
        probabilities.astype(jnp.bfloat16),
        window[:, head_dim:],
        preferred_element_type=jnp.float32,
    )
    attended = (mixed / total_mass[..., None]).astype(jnp.bfloat16).reshape(token_count, query_width)
    attended = passed_along(attended, "section", 1)
    return (layer_out[None], attended[None])


def solution(mesh):
    ep_size = mesh.shape["ep"]
    z_size = 4 if ep_size % 4 == 0 else 1
    x_size = 4 if ep_size % (z_size * 4) == 0 else 1
    split_mesh = jax.sharding.Mesh(
        mesh.devices.reshape(
            mesh.shape["section"], ep_size // (x_size * z_size), x_size, z_size
        ),
        ("section",) + EP,
    )
    in_specs = (
        P("section", EP, None),
        P("section", EP, None),
        P("section", EP, None),
        P("section", EP, None, None),
        P("section", EP, None, None),
        P("section", EP, None, None),
        P("section", EP, None),
        P("section", EP, None),
        P("section", None),
        P("section", None),
        P("section", EP),
    )
    out_specs = (P("section", EP, None), P("section", EP, None))

    return jax.shard_map(
        on_device, mesh=split_mesh, in_specs=in_specs, out_specs=out_specs, check_vma=False
    )
```

```python
import math

import jax
import jax.numpy as jnp
from jax import lax
from jax.sharding import PartitionSpec as P


OWNERS = 4
SEG_MOST = 512


EPSILON = 1e-06
ROPE_BASE = 1000000.0
FAR_INDEX = 1073741824
EP = ("ep_y", "ep_x", "ep_z")


def passed_along(block, axis, distance):
    devices = range(lax.axis_size(axis))
    route = [((i - distance) % len(devices), i) for i in devices]
    return lax.ppermute(block, axis, route)


def passed_along_2(value, axis, steps):
    count = lax.axis_size(axis)
    leading, last = (max(0, -steps), min(count, count - steps))
    return lax.ppermute(value, axis, [(source, source + steps) for source in range(leading, last)])


def rms_rows(values):
    return values * lax.rsqrt(jnp.mean(values * values, axis=-1, keepdims=True) + EPSILON)


def rotary(values, position):
    half_count = values.shape[-1] // 2
    frequency = ROPE_BASE ** (-(jnp.arange(half_count, dtype=jnp.float32) * 2.0) / values.shape[-1])
    angles = position.astype(jnp.float32)[:, None] * frequency[None, :]
    cosine = jnp.concatenate([jnp.cos(angles), jnp.cos(angles)], axis=-1)[:, None, :]
    sine = jnp.concatenate([jnp.sin(angles), jnp.sin(angles)], axis=-1)[:, None, :]
    turned = jnp.concatenate([-values[..., half_count:], values[..., :half_count]], axis=-1)
    return values * cosine + turned * sine


def feed_forward(row_block, gate_part, up_part, down_part):
    gate_proj = jnp.dot(row_block, gate_part, preferred_element_type=jnp.float32)
    up_proj = jnp.dot(row_block, up_part, preferred_element_type=jnp.float32)
    activated = (jax.nn.silu(gate_proj) * up_proj).astype(jnp.bfloat16)
    return jnp.dot(activated, down_part, preferred_element_type=jnp.float32)


def on_device(
    tokens,
    routes,
    router_weights,
    w_gate,
    w_up,
    w_down,
    w_query,
    w_keyval,
    gain_query,
    gain_key,
    segment_ids,
):
    device_count = lax.axis_size(EP)
    expert_count = device_count // OWNERS
    token_count = tokens.shape[1]
    model_width = tokens.shape[2]
    capacity = OWNERS * max(1, token_count // device_count)
    wide_tokens = tokens[0].astype(jnp.float32)
    normed = rms_rows(wide_tokens).astype(jnp.bfloat16)
    inside = routes[0] < expert_count
    has_route = jnp.any(inside, axis=-1)
    chosen = jnp.sum(jnp.where(inside, routes[0], 0), axis=-1)
    weight_kept = jnp.sum(jnp.where(inside, router_weights[0], 0.0), axis=-1)
    expert_ids = jnp.arange(expert_count, dtype=jnp.int32)
    member = ((chosen[:, None] == expert_ids[None, :]) & has_route[:, None]).astype(jnp.int32)
    rank_within = jnp.sum((jnp.cumsum(member, axis=0) - member) * member, axis=-1)
    slot_index = jnp.where(has_route, chosen * capacity + rank_within, -1)
    row_ids = jnp.arange(device_count * capacity, dtype=jnp.int32)
    row_expert = row_ids // (OWNERS * capacity)
    row_slot = row_ids % capacity
    placing = (
        (row_expert * capacity + row_slot)[:, None] == slot_index[None, :]
    ).astype(jnp.bfloat16)
    spread = (
        jnp.dot(placing, normed, preferred_element_type=jnp.float32)
        .astype(jnp.bfloat16)
        .reshape(device_count, capacity, model_width)
    )
    gate_part = w_gate[0, 0]
    up_part = w_up[0, 0]
    down_part = w_down[0, 0]
    next_query, next_keyval, segment_row, next_gain_query, next_gain_key = passed_along(
        (w_query[0], w_keyval[0], segment_ids[0], gain_query[0], gain_key[0]), "section", -1
    )
    first_index = lax.axis_index(EP) * token_count
    reach = (SEG_MOST - 1) // token_count + 1
    shard_rows = next_query.shape[0]
    per_row = -(-token_count // shard_rows)
    carried = jnp.pad(segment_row, (0, shard_rows * per_row - token_count)).reshape(
        shard_rows, per_row
    )
    carried = jnp.pad(carried.astype(jnp.bfloat16), ((0, 0), (0, 128 - per_row)))
    projection = jnp.concatenate([next_query, next_keyval, carried], axis=-1)
    projection = lax.all_gather(projection, EP[-1], axis=0, tiled=True)
    spread, projection = lax.optimization_barrier((spread, projection))
    received = lax.all_to_all(spread, EP, split_axis=0, concat_axis=0, tiled=True)
    received, projection = lax.optimization_barrier((received, projection))
    projection = lax.all_gather(projection, EP[:-1], axis=0, tiled=True)
    partial_out = feed_forward(
        received.reshape(-1, model_width), gate_part, up_part, down_part
    ).reshape(received.shape)
    returned_rows = lax.all_to_all(
        partial_out.astype(jnp.bfloat16), EP, split_axis=0, concat_axis=0, tiled=True
    )
    expert_out = jnp.dot(
        placing.T, returned_rows.reshape(-1, model_width), preferred_element_type=jnp.float32
    )
    layer_out = (wide_tokens + weight_kept[:, None] * expert_out).astype(jnp.bfloat16)
    lifted = rms_rows(layer_out.astype(jnp.float32)).astype(jnp.bfloat16)
    head_dim = gain_query.shape[-1]
    query_width = w_query.shape[-1]
    head_count = query_width // head_dim
    projected = jnp.dot(lifted, projection, preferred_element_type=jnp.float32)
    query_raw = projected[:, :query_width]
    keyval_raw = projected[:, query_width : query_width + 2 * head_dim]
    all_segments = (
        projection[:, query_width + 2 * head_dim :][:, :per_row]
        .astype(jnp.int32)
        .reshape(-1)[: device_count * token_count]
    )
    global_index = first_index + jnp.arange(token_count, dtype=jnp.int32)
    section_index = jnp.arange(device_count * token_count, dtype=jnp.int32)
    start_index = jnp.min(
        jnp.where(all_segments[None, :] == segment_row[:, None], section_index[None, :], FAR_INDEX),
        axis=1,
    )
    position = global_index - start_index
    key_index = (
        first_index - reach * token_count + jnp.arange((reach + 1) * token_count, dtype=jnp.int32)
    )
    query = rotary(
        rms_rows(query_raw.reshape(token_count, head_count, head_dim)) * next_gain_query, position
    ).astype(jnp.bfloat16)
    key_part = rotary(rms_rows(keyval_raw[:, None, :head_dim]) * next_gain_key, position)[
        :, 0
    ].astype(jnp.bfloat16)
    value_part = keyval_raw[:, head_dim:].astype(jnp.bfloat16)
    key_value = jnp.concatenate([key_part, value_part], axis=-1)
    earlier_pieces = []
    for distance in range(1, reach + 1):
        earlier_pieces.append(passed_along_2(key_value, EP, distance))
    window = jnp.concatenate(earlier_pieces[::-1] + [key_value], axis=0)
    score_scale = 1.0 / math.sqrt(head_dim)
    scores = (
        jnp.einsum(
            "thd,kd->thk", query, window[:, :head_dim], preferred_element_type=jnp.float32
        )
        * score_scale
    )
    allowed = (
        (key_index[None, :] >= start_index[:, None]) & (key_index[None, :] <= global_index[:, None])
    )[:, None, :]
    probabilities = jnp.where(allowed, jnp.exp(scores), 0.0)
    total_mass = jnp.sum(probabilities, axis=-1)
    mixed = jnp.einsum(
        "thk,kd->thd",
        probabilities.astype(jnp.bfloat16),
        window[:, head_dim:],
        preferred_element_type=jnp.float32,
    )
    attended = (mixed / total_mass[..., None]).astype(jnp.bfloat16).reshape(token_count, query_width)
    attended = passed_along(attended, "section", 1)
    return (layer_out[None], attended[None])


def solution(mesh):
    ep_size = mesh.shape["ep"]
    z_size = 4 if ep_size % 4 == 0 else 1
    x_size = 4 if ep_size % (z_size * 4) == 0 else 1
    split_mesh = jax.sharding.Mesh(
        mesh.devices.reshape(
            mesh.shape["section"], ep_size // (x_size * z_size), x_size, z_size
        ),
        ("section",) + EP,
    )
    in_specs = (
        P("section", EP, None),
        P("section", EP, None),
        P("section", EP, None),
        P("section", EP, None, None),
        P("section", EP, None, None),
        P("section", EP, None, None),
        P("section", EP, None),
        P("section", EP, None),
        P("section", None),
        P("section", None),
        P("section", EP),
    )
    out_specs = (P("section", EP, None), P("section", EP, None))

    return jax.shard_map(
        on_device, mesh=split_mesh, in_specs=in_specs, out_specs=out_specs, check_vma=False
    )
```

```python
import math

import jax
import jax.numpy as jnp
from jax import lax
from jax.sharding import PartitionSpec as P


OWNERS = 4
SEG_MOST = 512


EPSILON = 1e-06
ROPE_BASE = 1000000.0
FAR_INDEX = 1073741824
EP = ("ep_y", "ep_x", "ep_z")


def passed_along(block, axis, distance):
    devices = range(lax.axis_size(axis))
    route = [((i - distance) % len(devices), i) for i in devices]
    return lax.ppermute(block, axis, route)


def passed_along_2(value, axis, steps):
    count = lax.axis_size(axis)
    leading, last = (max(0, -steps), min(count, count - steps))
    return lax.ppermute(value, axis, [(source, source + steps) for source in range(leading, last)])


def rms_rows(values):
    return values * lax.rsqrt(jnp.mean(values * values, axis=-1, keepdims=True) + EPSILON)


def rotary(values, position):
    half_count = values.shape[-1] // 2
    frequency = ROPE_BASE ** (-(jnp.arange(half_count, dtype=jnp.float32) * 2.0) / values.shape[-1])
    angles = position.astype(jnp.float32)[:, None] * frequency[None, :]
    cosine = jnp.concatenate([jnp.cos(angles), jnp.cos(angles)], axis=-1)[:, None, :]
    sine = jnp.concatenate([jnp.sin(angles), jnp.sin(angles)], axis=-1)[:, None, :]
    turned = jnp.concatenate([-values[..., half_count:], values[..., :half_count]], axis=-1)
    return values * cosine + turned * sine


def feed_forward(row_block, gate_part, up_part, down_part):
    gate_proj = jnp.dot(row_block, gate_part, preferred_element_type=jnp.float32)
    up_proj = jnp.dot(row_block, up_part, preferred_element_type=jnp.float32)
    activated = (jax.nn.silu(gate_proj) * up_proj).astype(jnp.bfloat16)
    return jnp.dot(activated, down_part, preferred_element_type=jnp.float32)


def on_device(
    tokens,
    routes,
    router_weights,
    w_gate,
    w_up,
    w_down,
    w_query,
    w_keyval,
    gain_query,
    gain_key,
    segment_ids,
):
    device_count = lax.axis_size(EP)
    expert_count = device_count // OWNERS
    token_count = tokens.shape[1]
    model_width = tokens.shape[2]
    capacity = OWNERS * max(1, token_count // device_count)
    wide_tokens = tokens[0].astype(jnp.float32)
    normed = rms_rows(wide_tokens).astype(jnp.bfloat16)
    inside = routes[0] < expert_count
    has_route = jnp.any(inside, axis=-1)
    chosen = jnp.sum(jnp.where(inside, routes[0], 0), axis=-1)
    weight_kept = jnp.sum(jnp.where(inside, router_weights[0], 0.0), axis=-1)
    expert_ids = jnp.arange(expert_count, dtype=jnp.int32)
    member = ((chosen[:, None] == expert_ids[None, :]) & has_route[:, None]).astype(jnp.int32)
    rank_within = jnp.sum((jnp.cumsum(member, axis=0) - member) * member, axis=-1)
    slot_index = jnp.where(has_route, chosen * capacity + rank_within, -1)
    row_ids = jnp.arange(device_count * capacity, dtype=jnp.int32)
    row_expert = row_ids // (OWNERS * capacity)
    row_slot = row_ids % capacity
    placing = (
        (row_expert * capacity + row_slot)[:, None] == slot_index[None, :]
    ).astype(jnp.bfloat16)
    spread = (
        jnp.dot(placing, normed, preferred_element_type=jnp.float32)
        .astype(jnp.bfloat16)
        .reshape(device_count, capacity, model_width)
    )
    gate_part = w_gate[0, 0]
    up_part = w_up[0, 0]
    down_part = w_down[0, 0]
    next_query, next_keyval, segment_row, next_gain_query, next_gain_key = passed_along(
        (w_query[0], w_keyval[0], segment_ids[0], gain_query[0], gain_key[0]), "section", -1
    )
    first_index = lax.axis_index(EP) * token_count
    reach = (SEG_MOST - 1) // token_count + 1
    shard_rows = next_query.shape[0]
    per_row = -(-token_count // shard_rows)
    carried = jnp.pad(segment_row, (0, shard_rows * per_row - token_count)).reshape(
        shard_rows, per_row
    )
    carried = jnp.pad(carried.astype(jnp.bfloat16), ((0, 0), (0, 128 - per_row)))
    projection = jnp.concatenate([next_query, next_keyval, carried], axis=-1)
    projection = lax.all_gather(projection, EP[-1], axis=0, tiled=True)
    spread, projection = lax.optimization_barrier((spread, projection))
    projection = lax.all_gather(projection, EP[:-1], axis=0, tiled=True)
    received = lax.all_to_all(spread, EP, split_axis=0, concat_axis=0, tiled=True)
    half = capacity // 2
    placing_rows = placing.reshape(device_count, capacity, token_count)
    expert_out = 0.0
    for first, last in ((0, half), (half, capacity)):
        block = received[:, first:last]
        partial_out = feed_forward(
            block.reshape(-1, model_width), gate_part, up_part, down_part
        ).reshape(block.shape)
        returned_rows = lax.all_to_all(
            partial_out.astype(jnp.bfloat16), EP, split_axis=0, concat_axis=0, tiled=True
        )
        expert_out = expert_out + jnp.dot(
            placing_rows[:, first:last].reshape(-1, token_count).T,
            returned_rows.reshape(-1, model_width),
            preferred_element_type=jnp.float32,
        )
    layer_out = (wide_tokens + weight_kept[:, None] * expert_out).astype(jnp.bfloat16)
    lifted = rms_rows(layer_out.astype(jnp.float32)).astype(jnp.bfloat16)
    head_dim = gain_query.shape[-1]
    query_width = w_query.shape[-1]
    head_count = query_width // head_dim
    projected = jnp.dot(lifted, projection, preferred_element_type=jnp.float32)
    query_raw = projected[:, :query_width]
    keyval_raw = projected[:, query_width : query_width + 2 * head_dim]
    all_segments = (
        projection[:, query_width + 2 * head_dim :][:, :per_row]
        .astype(jnp.int32)
        .reshape(-1)[: device_count * token_count]
    )
    global_index = first_index + jnp.arange(token_count, dtype=jnp.int32)
    section_index = jnp.arange(device_count * token_count, dtype=jnp.int32)
    start_index = jnp.min(
        jnp.where(all_segments[None, :] == segment_row[:, None], section_index[None, :], FAR_INDEX),
        axis=1,
    )
    position = global_index - start_index
    key_index = (
        first_index - reach * token_count + jnp.arange((reach + 1) * token_count, dtype=jnp.int32)
    )
    query = rotary(
        rms_rows(query_raw.reshape(token_count, head_count, head_dim)) * next_gain_query, position
    ).astype(jnp.bfloat16)
    key_part = rotary(rms_rows(keyval_raw[:, None, :head_dim]) * next_gain_key, position)[
        :, 0
    ].astype(jnp.bfloat16)
    value_part = keyval_raw[:, head_dim:].astype(jnp.bfloat16)
    key_value = jnp.concatenate([key_part, value_part], axis=-1)
    earlier_pieces = []
    for distance in range(1, reach + 1):
        earlier_pieces.append(passed_along_2(key_value, EP, distance))
    window = jnp.concatenate(earlier_pieces[::-1] + [key_value], axis=0)
    score_scale = 1.0 / math.sqrt(head_dim)
    scores = (
        jnp.einsum(
            "thd,kd->thk", query, window[:, :head_dim], preferred_element_type=jnp.float32
        )
        * score_scale
    )
    allowed = (
        (key_index[None, :] >= start_index[:, None]) & (key_index[None, :] <= global_index[:, None])
    )[:, None, :]
    probabilities = jnp.where(allowed, jnp.exp(scores), 0.0)
    total_mass = jnp.sum(probabilities, axis=-1)
    mixed = jnp.einsum(
        "thk,kd->thd",
        probabilities.astype(jnp.bfloat16),
        window[:, head_dim:],
        preferred_element_type=jnp.float32,
    )
    attended = (mixed / total_mass[..., None]).astype(jnp.bfloat16).reshape(token_count, query_width)
    attended = passed_along(attended, "section", 1)
    return (layer_out[None], attended[None])


def solution(mesh):
    ep_size = mesh.shape["ep"]
    z_size = 4 if ep_size % 4 == 0 else 1
    x_size = 4 if ep_size % (z_size * 4) == 0 else 1
    split_mesh = jax.sharding.Mesh(
        mesh.devices.reshape(
            mesh.shape["section"], ep_size // (x_size * z_size), x_size, z_size
        ),
        ("section",) + EP,
    )
    in_specs = (
        P("section", EP, None),
        P("section", EP, None),
        P("section", EP, None),
        P("section", EP, None, None),
        P("section", EP, None, None),
        P("section", EP, None, None),
        P("section", EP, None),
        P("section", EP, None),
        P("section", None),
        P("section", None),
        P("section", EP),
    )
    out_specs = (P("section", EP, None), P("section", EP, None))

    return jax.shard_map(
        on_device, mesh=split_mesh, in_specs=in_specs, out_specs=out_specs, check_vma=False
    )
```

```python
import math

import jax
import jax.numpy as jnp
from jax import lax
from jax.sharding import PartitionSpec as P


OWNERS = 4
SEG_MOST = 512


EPSILON = 1e-06
ROPE_BASE = 1000000.0
FAR_INDEX = 1073741824
EP = ("ep_y", "ep_x", "ep_z")


def passed_along(block, axis, distance):
    devices = range(lax.axis_size(axis))
    route = [((i - distance) % len(devices), i) for i in devices]
    return lax.ppermute(block, axis, route)


def passed_along_2(value, axis, steps):
    count = lax.axis_size(axis)
    leading, last = (max(0, -steps), min(count, count - steps))
    return lax.ppermute(value, axis, [(source, source + steps) for source in range(leading, last)])


def rms_rows(values):
    return values * lax.rsqrt(jnp.mean(values * values, axis=-1, keepdims=True) + EPSILON)


def rotary(values, position):
    half_count = values.shape[-1] // 2
    frequency = ROPE_BASE ** (-(jnp.arange(half_count, dtype=jnp.float32) * 2.0) / values.shape[-1])
    angles = position.astype(jnp.float32)[:, None] * frequency[None, :]
    cosine = jnp.concatenate([jnp.cos(angles), jnp.cos(angles)], axis=-1)[:, None, :]
    sine = jnp.concatenate([jnp.sin(angles), jnp.sin(angles)], axis=-1)[:, None, :]
    turned = jnp.concatenate([-values[..., half_count:], values[..., :half_count]], axis=-1)
    return values * cosine + turned * sine


def feed_forward(row_block, gate_part, up_part, down_part):
    gate_proj = jnp.dot(row_block, gate_part, preferred_element_type=jnp.float32)
    up_proj = jnp.dot(row_block, up_part, preferred_element_type=jnp.float32)
    activated = (jax.nn.silu(gate_proj) * up_proj).astype(jnp.bfloat16)
    return jnp.dot(activated, down_part, preferred_element_type=jnp.float32)


def on_device(
    tokens,
    routes,
    router_weights,
    w_gate,
    w_up,
    w_down,
    w_query,
    w_keyval,
    gain_query,
    gain_key,
    segment_ids,
):
    device_count = lax.axis_size(EP)
    expert_count = device_count // OWNERS
    token_count = tokens.shape[1]
    model_width = tokens.shape[2]
    capacity = OWNERS * max(1, token_count // device_count)
    wide_tokens = tokens[0].astype(jnp.float32)
    normed = rms_rows(wide_tokens).astype(jnp.bfloat16)
    inside = routes[0] < expert_count
    has_route = jnp.any(inside, axis=-1)
    chosen = jnp.sum(jnp.where(inside, routes[0], 0), axis=-1)
    weight_kept = jnp.sum(jnp.where(inside, router_weights[0], 0.0), axis=-1)
    expert_ids = jnp.arange(expert_count, dtype=jnp.int32)
    member = ((chosen[:, None] == expert_ids[None, :]) & has_route[:, None]).astype(jnp.int32)
    rank_within = jnp.sum((jnp.cumsum(member, axis=0) - member) * member, axis=-1)
    slot_index = jnp.where(has_route, chosen * capacity + rank_within, -1)
    row_ids = jnp.arange(device_count * capacity, dtype=jnp.int32)
    row_expert = row_ids // (OWNERS * capacity)
    row_slot = row_ids % capacity
    placing = (
        (row_expert * capacity + row_slot)[:, None] == slot_index[None, :]
    ).astype(jnp.bfloat16)
    spread = (
        jnp.dot(placing, normed, preferred_element_type=jnp.float32)
        .astype(jnp.bfloat16)
        .reshape(device_count, capacity, model_width)
    )
    gate_part = w_gate[0, 0]
    up_part = w_up[0, 0]
    down_part = w_down[0, 0]
    next_query, next_keyval, segment_row, next_gain_query, next_gain_key = passed_along(
        (w_query[0], w_keyval[0], segment_ids[0], gain_query[0], gain_key[0]), "section", -1
    )
    first_index = lax.axis_index(EP) * token_count
    reach = (SEG_MOST - 1) // token_count + 1
    shard_rows = next_query.shape[0]
    per_row = -(-token_count // shard_rows)
    carried = jnp.pad(segment_row, (0, shard_rows * per_row - token_count)).reshape(
        shard_rows, per_row
    )
    carried = jnp.pad(carried.astype(jnp.bfloat16), ((0, 0), (0, 128 - per_row)))
    projection = jnp.concatenate([next_query, next_keyval, carried], axis=-1)
    projection = lax.all_gather(projection, EP[-1], axis=0, tiled=True)
    spread, projection = lax.optimization_barrier((spread, projection))
    projection = lax.all_gather(projection, EP[:-1], axis=0, tiled=True)
    received = lax.all_to_all(spread, EP, split_axis=0, concat_axis=0, tiled=True)
    partial_out = feed_forward(
        received.reshape(-1, model_width), gate_part, up_part, down_part
    ).reshape(received.shape)
    returned_rows = lax.all_to_all(
        partial_out.astype(jnp.bfloat16), EP, split_axis=0, concat_axis=0, tiled=True
    )
    expert_out = jnp.dot(
        placing.T, returned_rows.reshape(-1, model_width), preferred_element_type=jnp.float32
    )
    layer_out = (wide_tokens + weight_kept[:, None] * expert_out).astype(jnp.bfloat16)
    lifted = rms_rows(layer_out.astype(jnp.float32)).astype(jnp.bfloat16)
    head_dim = gain_query.shape[-1]
    query_width = w_query.shape[-1]
    head_count = query_width // head_dim
    projected = jnp.dot(lifted, projection, preferred_element_type=jnp.float32)
    query_raw = projected[:, :query_width]
    keyval_raw = projected[:, query_width : query_width + 2 * head_dim]
    all_segments = (
        projection[:, query_width + 2 * head_dim :][:, :per_row]
        .astype(jnp.int32)
        .reshape(-1)[: device_count * token_count]
    )
    global_index = first_index + jnp.arange(token_count, dtype=jnp.int32)
    section_index = jnp.arange(device_count * token_count, dtype=jnp.int32)
    start_index = jnp.min(
        jnp.where(all_segments[None, :] == segment_row[:, None], section_index[None, :], FAR_INDEX),
        axis=1,
    )
    position = global_index - start_index
    key_index = (
        first_index - reach * token_count + jnp.arange((reach + 1) * token_count, dtype=jnp.int32)
    )
    query = rotary(
        rms_rows(query_raw.reshape(token_count, head_count, head_dim)) * next_gain_query, position
    ).astype(jnp.bfloat16)
    key_part = rotary(rms_rows(keyval_raw[:, None, :head_dim]) * next_gain_key, position)[
        :, 0
    ].astype(jnp.bfloat16)
    value_part = keyval_raw[:, head_dim:].astype(jnp.bfloat16)
    key_value = jnp.concatenate([key_part, value_part], axis=-1)
    earlier_pieces = []
    for distance in range(1, reach + 1):
        earlier_pieces.append(passed_along_2(key_value, EP, distance))
    window = jnp.concatenate(earlier_pieces[::-1] + [key_value], axis=0)
    score_scale = 1.0 / math.sqrt(head_dim)
    allowed = (
        (key_index[None, :] >= start_index[:, None]) & (key_index[None, :] <= global_index[:, None])
    )[:, None, :]
    head_half = head_count // 2
    handed = []
    for first in (0, head_half):
        scores = (
            jnp.einsum(
                "thd,kd->thk",
                query[:, first : first + head_half],
                window[:, :head_dim],
                preferred_element_type=jnp.float32,
            )
            * score_scale
        )
        probabilities = jnp.where(allowed, jnp.exp(scores), 0.0)
        total_mass = jnp.sum(probabilities, axis=-1)
        mixed = jnp.einsum(
            "thk,kd->thd",
            probabilities.astype(jnp.bfloat16),
            window[:, head_dim:],
            preferred_element_type=jnp.float32,
        )
        part = (mixed / total_mass[..., None]).astype(jnp.bfloat16)
        handed.append(passed_along(part.reshape(token_count, -1), "section", 1))
    attended = jnp.concatenate(handed, axis=-1)
    return (layer_out[None], attended[None])


def solution(mesh):
    ep_size = mesh.shape["ep"]
    z_size = 4 if ep_size % 4 == 0 else 1
    x_size = 4 if ep_size % (z_size * 4) == 0 else 1
    split_mesh = jax.sharding.Mesh(
        mesh.devices.reshape(
            mesh.shape["section"], ep_size // (x_size * z_size), x_size, z_size
        ),
        ("section",) + EP,
    )
    in_specs = (
        P("section", EP, None),
        P("section", EP, None),
        P("section", EP, None),
        P("section", EP, None, None),
        P("section", EP, None, None),
        P("section", EP, None, None),
        P("section", EP, None),
        P("section", EP, None),
        P("section", None),
        P("section", None),
        P("section", EP),
    )
    out_specs = (P("section", EP, None), P("section", EP, None))

    return jax.shard_map(
        on_device, mesh=split_mesh, in_specs=in_specs, out_specs=out_specs, check_vma=False
    )
```
